128 devices in a mesh: pp: 8 (over x, y_hi), ep: 16 (over z, y_lo, core).
Axes of the slice: x: 4, y: 4 (y_hi: 2, y_lo: 2; y = y_hi * 2 + y_lo), z: 4, core: 2. Of those that a mesh axis runs over, the one named last changes fastest.
Arguments:
- prev_out: bfloat16 [8, 2048, 7168], P('pp', 'ep'), may hold values from -6 to 6
- fwd_experts: int32 [8, 2048, 2], P('pp', 'ep'), may hold values from 0 to 7, all different within a row; in each aligned block of 128 rows (0 to 127, 128 to 255, ..., all dimensions but the last counted through in order) at most 48 rows name the same one
- expert_weights: bfloat16 [8, 16, 7168, 1024], P('pp', 'ep'), may hold values from -0.0625 to 0.0625
- bwd_experts: int32 [8, 2048, 2], P('pp', 'ep'), may hold values from 0 to 7, all different within a row; in each aligned block of 128 rows (0 to 127, 128 to 255, ..., all dimensions but the last counted through in order) at most 48 rows name the same one
- grad_hidden: bfloat16 [8, 16, 16, 48, 512], P('pp', 'ep'), may hold values from -6 to 6
- saved_pre: bfloat16 [8, 16, 16, 48, 1024], P('pp', 'ep'), may hold values from -6 to 6
Outputs:
- hidden_out: bfloat16 [8, 16, 16, 48, 512], P('pp', 'ep')
- grad_rows: bfloat16 [8, 2048, 7168], P('pp', 'ep')
The draws below stay inside these ranges and needn't reach their ends.
Inputs may be any that keep to these rules, and one draw needn't show every extreme that they name: `fwd_experts`: each row names 2 different experts, and within the 128 rows of one device no expert is named more than 48 times. `bwd_experts`: each row names 2 different experts, and within the 128 rows of one device no expert is named more than 48 times.
All inputs are finite; a program needn't handle non-finite values.
Results may differ from the reference program's by a relative error of at most 0.0066.
Values may be sent and summed in bfloat16 or wider, within the bound.
No kernel may reach another device: no remote copies, remote signals or barrier semaphores. Data moves between devices by JAX's collectives and lax.ppermute only.
A program may use at most 128 MiB of HBM per device.

```python
import math
from functools import partial
import jax
import jax.numpy as jnp
import numpy as np
from jax import lax

D = 7168
HID_DEV = 512
TOP = 2
SECTIONS = 8
EXPERTS = 8
TOK_DEV = 128
TOKENS = 2048
CAP = 48
N_EP = 16


def steps_of(rng, shape, split, least, high):
    gain = 1.0
    for axis_at, blocks in split:
        draws = jax.random.uniform(jax.random.fold_in(jax.random.fold_in(rng, 6), axis_at), (blocks,), jnp.float32, least / len(split), high / len(split))
        gain = gain * jnp.repeat(jnp.exp(draws), shape[axis_at] // blocks).reshape((-1,) + (1,) * (len(shape) - 1 - axis_at))
    return gain


def shared_out(own_key, own, number, rows, number_of, top, limit, lean):
    sequence = jax.random.permutation(own_key, number_of)
    packed, common = load_shares(number_of, rows * top, limit, lean, True), load_shares(number_of, rows * top, limit, lean, False)
    places = jnp.arange(number_of)

    def named(lengths, offset_by):
        used = int((lengths > 0).sum())
        fixed = max(1, used // 4)
        passed = fixed + (places - fixed + offset_by * (used - fixed)) % max(1, number_of - fixed)
        return jnp.zeros((number_of,), jnp.int32).at[sequence[jnp.where(places < fixed, places, passed)]].set(jnp.asarray(lengths, jnp.int32))

    lengths = jnp.where(number % 4 == 0, named(packed, number // 4), named(common, number - number // 4 - 1))
    mixed = jax.random.permutation(jax.random.fold_in(own, 3), number_of)
    donor, sink = mixed[0:number_of // 2 * 2:2], mixed[1:number_of // 2 * 2:2]
    room = jnp.minimum(lengths[donor] - 1, limit - lengths[sink]) // 2
    room = jnp.where((donor == sequence[0]) | (sink == sequence[0]) | (lengths[sink] == 0), 0, jnp.maximum(room, 0))
    passed = jax.random.randint(jax.random.fold_in(own, 4), (number_of // 2,), 0, 1 << 20) % (room + 1)
    lengths = lengths.at[donor].add(-passed).at[sink].add(passed)
    items = jnp.searchsorted(jnp.cumsum(lengths), jnp.arange(rows * top), side="right").astype(jnp.int32)
    grid = items.reshape(top, rows).T
    grid = grid[jax.random.permutation(jax.random.fold_in(own, 1), rows)]
    offset_by = jax.random.randint(jax.random.fold_in(own, 2), (rows, 1), 0, top)
    return jnp.take_along_axis(grid, (jnp.arange(top)[None, :] + offset_by) % top, axis=1)


def load_shares(count, total, bound, slope, full):
    weights = [(1 << 20) // math.isqrt(grade ** slope) + 1 for grade in range(1, count + 1)]
    largest = bound if full else min(bound, max(-(-total // count), total * weights[0] // sum(weights)))
    least = 1 if total - largest >= count - 1 else 0
    holding, surplus = [largest] + [least] * (count - 1), total - largest - least * (count - 1)
    while surplus > 0:
        candidates = [i for i in range(1, count) if holding[i] < largest] or [i for i in range(1, count) if holding[i] < bound]
        mass, budget = sum([weights[i] for i in candidates]), surplus
        for i in candidates:
            more = min(bound - holding[i], max(1, budget * weights[i] // mass), surplus)
            holding[i] = holding[i] + more
            surplus = surplus - more
    return np.array(holding)


def centred(own_key, extent, scale, limit, split=(), held_as=jnp.bfloat16):
    array = scale * jax.random.normal(own_key, extent, jnp.float32)
    if split:
        array = array * steps_of(own_key, extent, split, -0.22, 0.18)
    return jnp.clip(array, -limit, limit).astype(held_as)


def setup_inputs(seed: int = 0) -> dict:
    seeds = jax.random.split(jax.random.key(seed), 7)
    prev_out = centred(seeds[0], (SECTIONS, TOKENS, D), 1.0, 6.0, ((0, 8), (1, 16)))
    fwd_experts_keys = jax.random.split(jax.random.fold_in(seeds[1], 1), SECTIONS * TOKENS // TOK_DEV)
    fwd_experts_turns = jax.random.permutation(jax.random.fold_in(seeds[1], 3), SECTIONS * TOKENS // TOK_DEV)
    fwd_experts = jax.vmap(lambda own, number: shared_out(jax.random.fold_in(seeds[1], 2), own, number, TOK_DEV, EXPERTS, TOP, CAP, 2))(fwd_experts_keys, fwd_experts_turns).reshape((SECTIONS, TOKENS, TOP))
    expert_weights = centred(seeds[2], (SECTIONS, N_EP, D, 2 * HID_DEV), D ** -0.5, 0.0625, ((0, 8), (1, 16)))
    bwd_experts_keys = jax.random.split(jax.random.fold_in(seeds[3], 1), SECTIONS * TOKENS // TOK_DEV)
    bwd_experts_turns = jax.random.permutation(jax.random.fold_in(seeds[3], 3), SECTIONS * TOKENS // TOK_DEV)
    bwd_experts = jax.vmap(lambda own, number: shared_out(jax.random.fold_in(seeds[3], 2), own, number, TOK_DEV, EXPERTS, TOP, CAP, 2))(bwd_experts_keys, bwd_experts_turns).reshape((SECTIONS, TOKENS, TOP))
    grad_hidden = centred(seeds[4], (SECTIONS, N_EP, N_EP, CAP, HID_DEV), 1.0, 6.0, ((0, 8), (1, 16)))
    saved_pre = centred(seeds[5], (SECTIONS, N_EP, N_EP, CAP, 2 * HID_DEV), 1.0, 6.0, ((0, 8), (1, 16)))
    return dict(prev_out=prev_out, fwd_experts=fwd_experts, expert_weights=expert_weights, bwd_experts=bwd_experts, grad_hidden=grad_hidden, saved_pre=saved_pre)


def slot_table(route_ids, expert_count, capacity):
    token_count, choice_count = route_ids.shape
    flattened = route_ids.reshape(token_count * choice_count)
    onehot = (flattened[:, None] == jnp.arange(expert_count, dtype=jnp.int32)[None, :]).astype(jnp.int32)
    earlier = jnp.cumsum(onehot, axis=0) - onehot
    slot_index = jnp.sum(earlier * onehot, axis=1)
    slot_match = (slot_index[:, None] == jnp.arange(capacity, dtype=jnp.int32)[None, :]).astype(jnp.float32)
    expert_match = onehot.astype(jnp.float32)
    joined = jnp.einsum('re,rc->rec', expert_match, slot_match).reshape(token_count, choice_count, expert_count, capacity)
    return jnp.transpose(jnp.sum(joined, axis=1), (1, 2, 0))


def swiglu_forward(received, weights):
    hid_units = weights.shape[1] // 2
    projected = jnp.einsum('scd,dh->sch', received.astype(jnp.float32), weights.astype(jnp.float32))
    return (jax.nn.silu(projected[..., :hid_units]) * projected[..., hid_units:]).astype(jnp.bfloat16)


def swiglu_backward(upstream, saved):
    hid_units = upstream.shape[-1]
    pre_float = saved.astype(jnp.float32)
    gate_pre = pre_float[..., :hid_units]
    up_pre = pre_float[..., hid_units:]
    sigmoid_gate = jax.nn.sigmoid(gate_pre)
    upstream_float = upstream.astype(jnp.float32)
    grad_gate = upstream_float * up_pre * sigmoid_gate * (1.0 + gate_pre * (1.0 - sigmoid_gate))
    grad_up = upstream_float * gate_pre * sigmoid_gate
    return jnp.concatenate([grad_gate, grad_up], axis=-1).astype(jnp.bfloat16)


def reference(prev_out, fwd_experts, expert_weights, bwd_experts, grad_hidden, saved_pre):
    make_tables = jax.vmap(partial(slot_table, expert_count=EXPERTS, capacity=CAP))
    rows_in = jnp.roll(prev_out, 1, axis=0)

    def section_forward(section_args):
        section_rows, route_ids, weights = section_args
        blocks = section_rows.reshape(N_EP, TOK_DEV, D).astype(jnp.float32)
        tables = make_tables(route_ids.reshape(N_EP, TOK_DEV, TOP))
        picked = lax.optimization_barrier(jnp.einsum('sect,std->secd', tables, blocks).astype(jnp.bfloat16))

        def one_shard(shard_index):
            received = jnp.take(picked, shard_index // 2, axis=1)
            return swiglu_forward(received, jnp.take(weights, shard_index, axis=0))

        return lax.map(one_shard, jnp.arange(N_EP, dtype=jnp.int32))

    hidden_out = lax.map(section_forward, (rows_in, fwd_experts, expert_weights))

    def section_backward(section_args):
        route_ids, weights, upstream, saved = section_args
        tables = make_tables(route_ids.reshape(N_EP, TOK_DEV, TOP))

        def shard_partial(shard_index):
            grad_pre = lax.optimization_barrier(swiglu_backward(jnp.take(upstream, shard_index, axis=0), jnp.take(saved, shard_index, axis=0)))
            shard_weights = jnp.take(weights, shard_index, axis=0).astype(jnp.float32)
            product = jnp.einsum('sch,dh->scd', grad_pre.astype(jnp.float32), shard_weights)
            return lax.optimization_barrier(product.astype(jnp.bfloat16))

        def one_expert(running, expert):
            leading = shard_partial(2 * expert).astype(jnp.float32)
            trailing = shard_partial(2 * expert + 1).astype(jnp.float32)
            pair_sum = lax.optimization_barrier((leading + trailing).astype(jnp.bfloat16)).astype(jnp.float32)
            expert_table = jnp.take(tables, expert, axis=1)
            return running + jnp.einsum('sct,scd->std', expert_table, pair_sum), None

        accumulated, _ = lax.scan(one_expert, jnp.zeros((N_EP, TOK_DEV, D), jnp.float32), jnp.arange(EXPERTS, dtype=jnp.int32))
        return accumulated.astype(jnp.bfloat16).reshape(N_EP * TOK_DEV, D)

    grad_in = lax.map(section_backward, (bwd_experts, expert_weights, grad_hidden, saved_pre))
    return hidden_out, jnp.roll(grad_in, -1, axis=0)
```

```python
import numpy as np
import jax
import jax.numpy as jnp
from jax import lax
from jax.sharding import Mesh
from jax.sharding import PartitionSpec as P

PP = ("x", "yhi")
EP = ("z", "ylo", "core")
CHIPS = ("z", "ylo")
RING = ("x", "yhi", "ylo")


def ring_route(sections, distance):
    route = []
    for p in range(sections):
        for lo in range(2):
            route.append((p * 2 + lo, ((p + distance) % sections) * 2 + (1 - lo)))
    return route


def swap_ylo(block):
    return lax.ppermute(block, "ylo", [(0, 1), (1, 0)])


def slot_table(route_ids, expert_count, capacity):
    token_count, choice_count = route_ids.shape
    flattened = route_ids.reshape(token_count * choice_count)
    onehot = (flattened[:, None] == jnp.arange(expert_count, dtype=jnp.int32)[None, :]).astype(
        jnp.int32
    )
    earlier = jnp.cumsum(onehot, axis=0) - onehot
    slot_index = jnp.sum(earlier * onehot, axis=1)
    slot_match = (slot_index[:, None] == jnp.arange(capacity, dtype=jnp.int32)[None, :]).astype(
        jnp.float32
    )
    expert_match = onehot.astype(jnp.float32)
    joined = jnp.einsum("re,rc->rec", expert_match, slot_match).reshape(
        token_count, choice_count, expert_count, capacity
    )
    return jnp.transpose(jnp.sum(joined, axis=1), (1, 2, 0))


def swiglu_backward(upstream, saved):
    hid_units = upstream.shape[-1]
    pre_float = saved.astype(jnp.float32)
    gate_pre = pre_float[..., :hid_units]
    up_pre = pre_float[..., hid_units:]
    sigmoid_gate = jax.nn.sigmoid(gate_pre)
    upstream_float = upstream.astype(jnp.float32)
    grad_gate = upstream_float * up_pre * sigmoid_gate * (1.0 + gate_pre * (1.0 - sigmoid_gate))
    grad_up = upstream_float * gate_pre * sigmoid_gate
    return jnp.concatenate([grad_gate, grad_up], axis=-1).astype(jnp.bfloat16)


def make_shards(sections, zs):
    def shards(prev_out, fwd_experts, expert_weights, bwd_experts, grad_hidden, saved_pre):
        experts = 2 * zs
        capacity = grad_hidden.shape[3]
        hid_units = grad_hidden.shape[4]
        model_width = prev_out.shape[2]
        weights = expert_weights[0, 0]
        core = lax.axis_index("core")

        rows = lax.ppermute(prev_out[0], RING, ring_route(sections, 1))
        fwd_ids = swap_ylo(fwd_experts[0])
        fwd_table = slot_table(fwd_ids, experts, capacity).astype(jnp.bfloat16)
        picked = jnp.einsum(
            "ect,td->ecd", fwd_table, rows, preferred_element_type=jnp.float32
        ).astype(jnp.bfloat16)
        arrived = lax.all_to_all(picked, CHIPS, split_axis=0, concat_axis=0, tiled=True)
        both = lax.all_gather(arrived, "core", axis=0, tiled=False)
        projected = jnp.einsum(
            "scd,dh->sch",
            both.reshape(2 * experts, capacity, model_width),
            weights,
            preferred_element_type=jnp.float32,
        )
        hidden = (jax.nn.silu(projected[..., :hid_units]) * projected[..., hid_units:]).astype(
            jnp.bfloat16
        )
        hidden = hidden.reshape(2, zs, 2, capacity, hid_units)[:, :, ::-1]
        hidden = jnp.transpose(hidden, (1, 2, 0, 3, 4)).reshape(2 * experts, capacity, hid_units)

        upstream = grad_hidden[0, 0].reshape(zs, 2, 2, capacity, hid_units)
        saved = saved_pre[0, 0].reshape(zs, 2, 2, capacity, 2 * hid_units)
        keep_pre = swiglu_backward(
            lax.dynamic_index_in_dim(upstream, core, axis=2, keepdims=False),
            lax.dynamic_index_in_dim(saved, core, axis=2, keepdims=False),
        )
        send_pre = swiglu_backward(
            lax.dynamic_index_in_dim(upstream, 1 - core, axis=2, keepdims=False),
            lax.dynamic_index_in_dim(saved, 1 - core, axis=2, keepdims=False),
        )
        send_part = jnp.einsum(
            "zych,dh->zycd", send_pre, weights, preferred_element_type=jnp.float32
        ).astype(jnp.bfloat16)
        other_part = lax.ppermute(send_part, "core", [(0, 1), (1, 0)])
        keep_part = jnp.einsum(
            "zych,dh->zycd", keep_pre, weights, preferred_element_type=jnp.float32
        ).astype(jnp.bfloat16)
        pair_sum = (keep_part.astype(jnp.float32) + other_part.astype(jnp.float32)).astype(
            jnp.bfloat16
        )
        outgoing = pair_sum[:, ::-1].reshape(experts, capacity, model_width)
        returned = lax.all_to_all(outgoing, CHIPS, split_axis=0, concat_axis=0, tiled=True)
        bwd_ids = swap_ylo(bwd_experts[0])
        bwd_table = slot_table(bwd_ids, experts, capacity).astype(jnp.bfloat16)
        grad_in = jnp.einsum(
            "ect,ecd->td", bwd_table, returned, preferred_element_type=jnp.float32
        ).astype(jnp.bfloat16)
        grad_rows = lax.ppermute(grad_in, RING, ring_route(sections, -1))
        return (hidden[None, None], grad_rows[None])

    return shards


def solution(mesh):
    sections = mesh.shape["pp"]
    groups = mesh.shape["ep"]
    zs = groups // 4
    devices = np.asarray(mesh.devices).reshape(sections // 2, 2, zs, 2, 2)
    fine = Mesh(devices, PP + EP)
    placed = (
        P(PP, EP, None),
        P(PP, EP, None),
        P(PP, EP, None, None),
        P(PP, EP, None),
        P(PP, EP, None, None, None),
        P(PP, EP, None, None, None),
    )
    return jax.shard_map(
        make_shards(sections, zs),
        mesh=fine,
        in_specs=placed,
        out_specs=(P(PP, EP, None, None, None), P(PP, EP, None)),
        check_vma=False,
    )
```

```python
import numpy as np
import jax
import jax.numpy as jnp
from jax import lax
from jax.sharding import Mesh
from jax.sharding import PartitionSpec as P

PP = ("x", "yhi")
EP = ("z", "ylo", "core")
CHIPS = ("z", "ylo")
RING = ("x", "yhi", "ylo")


def ring_route(sections, distance):
    route = []
    for p in range(sections):
        for lo in range(2):
            route.append((p * 2 + lo, ((p + distance) % sections) * 2 + (1 - lo)))
    return route


def swap_ylo(block):
    return lax.ppermute(block, "ylo", [(0, 1), (1, 0)])


def slot_table(route_ids, expert_count, capacity):
    token_count, choice_count = route_ids.shape
    flattened = route_ids.reshape(token_count * choice_count)
    onehot = (flattened[:, None] == jnp.arange(expert_count, dtype=jnp.int32)[None, :]).astype(
        jnp.int32
    )
    earlier = jnp.cumsum(onehot, axis=0) - onehot
    slot_index = jnp.sum(earlier * onehot, axis=1)
    slot_match = (slot_index[:, None] == jnp.arange(capacity, dtype=jnp.int32)[None, :]).astype(
        jnp.float32
    )
    expert_match = onehot.astype(jnp.float32)
    joined = jnp.einsum("re,rc->rec", expert_match, slot_match).reshape(
        token_count, choice_count, expert_count, capacity
    )
    return jnp.transpose(jnp.sum(joined, axis=1), (1, 2, 0))


def swiglu_backward(upstream, saved):
    hid_units = upstream.shape[-1]
    pre_float = saved.astype(jnp.float32)
    gate_pre = pre_float[..., :hid_units]
    up_pre = pre_float[..., hid_units:]
    sigmoid_gate = jax.nn.sigmoid(gate_pre)
    upstream_float = upstream.astype(jnp.float32)
    grad_gate = upstream_float * up_pre * sigmoid_gate * (1.0 + gate_pre * (1.0 - sigmoid_gate))
    grad_up = upstream_float * gate_pre * sigmoid_gate
    return jnp.concatenate([grad_gate, grad_up], axis=-1).astype(jnp.bfloat16)


def chip_route(chips, k):
    return [(j, j ^ k) for j in range(chips)]


def make_shards(sections, zs):
    chips = 2 * zs

    def shards(prev_out, fwd_experts, expert_weights, bwd_experts, grad_hidden, saved_pre):
        experts = chips
        capacity = grad_hidden.shape[3]
        hid_units = grad_hidden.shape[4]
        model_width = prev_out.shape[2]
        weights = expert_weights[0, 0]
        core = lax.axis_index("core")
        me = lax.axis_index("z") * 2 + lax.axis_index("ylo")
        peer = me ^ jnp.arange(chips, dtype=jnp.int32)
        worked = (peer // 2) * 4 + (1 - peer % 2) * 2

        ids = swap_ylo(jnp.concatenate([fwd_experts[0], bwd_experts[0]], axis=1))
        fwd_ids = ids[:, : fwd_experts.shape[2]]
        bwd_ids = ids[:, fwd_experts.shape[2] :]

        rows = lax.ppermute(prev_out[0], RING, ring_route(sections, 1))

        order = jnp.concatenate([worked + core, worked + 1 - core])
        upstream = jnp.take(grad_hidden[0, 0], order, axis=0)
        saved = jnp.take(saved_pre[0, 0], order, axis=0)
        grad_pre = swiglu_backward(upstream, saved).reshape(2, chips, capacity, 2 * hid_units)
        partial_rows = jnp.einsum(
            "kech,dh->kecd", grad_pre, weights, preferred_element_type=jnp.float32
        ).astype(jnp.bfloat16)
        other_part = lax.ppermute(partial_rows[1], "core", [(0, 1), (1, 0)])
        pair_sum = (partial_rows[0].astype(jnp.float32) + other_part.astype(jnp.float32)).astype(
            jnp.bfloat16
        )
        returned = [pair_sum[0]] + [
            lax.ppermute(pair_sum[k], CHIPS, chip_route(chips, k)) for k in range(1, chips)
        ]
        rows, _ = lax.optimization_barrier((rows, pair_sum))

        fwd_table = slot_table(fwd_ids, experts, capacity).astype(jnp.bfloat16)
        fwd_table = jnp.take(fwd_table, peer, axis=0)
        picked = jnp.einsum(
            "ect,td->ecd", fwd_table, rows, preferred_element_type=jnp.float32
        ).astype(jnp.bfloat16)
        arrived = jnp.stack(
            [picked[0]]
            + [lax.ppermute(picked[k], CHIPS, chip_route(chips, k)) for k in range(1, chips)]
        )
        both = lax.all_gather(arrived, "core", axis=0, tiled=False)
        projected = jnp.einsum(
            "scd,dh->sch",
            both.reshape(2 * experts, capacity, model_width),
            weights,
            preferred_element_type=jnp.float32,
        )
        hidden = (jax.nn.silu(projected[..., :hid_units]) * projected[..., hid_units:]).astype(
            jnp.bfloat16
        )
        blocks = jnp.arange(2 * experts, dtype=jnp.int32)
        chip_of = (blocks // 4) * 2 + (1 - (blocks // 2) % 2)
        hidden = jnp.take(hidden, (blocks % 2) * chips + (chip_of ^ me), axis=0)

        bwd_table = slot_table(bwd_ids, experts, capacity).astype(jnp.bfloat16)
        bwd_table = jnp.take(bwd_table, peer, axis=0)
        grad_in = jnp.einsum(
            "ect,ecd->td", bwd_table, jnp.stack(returned), preferred_element_type=jnp.float32
        ).astype(jnp.bfloat16)
        grad_rows = lax.ppermute(grad_in, RING, ring_route(sections, -1))
        return (hidden[None, None], grad_rows[None])

    return shards


def solution(mesh):
    sections = mesh.shape["pp"]
    groups = mesh.shape["ep"]
    zs = groups // 4
    devices = np.asarray(mesh.devices).reshape(sections // 2, 2, zs, 2, 2)
    fine = Mesh(devices, PP + EP)
    placed = (
        P(PP, EP, None),
        P(PP, EP, None),
        P(PP, EP, None, None),
        P(PP, EP, None),
        P(PP, EP, None, None, None),
        P(PP, EP, None, None, None),
    )
    return jax.shard_map(
        make_shards(sections, zs),
        mesh=fine,
        in_specs=placed,
        out_specs=(P(PP, EP, None, None, None), P(PP, EP, None)),
        check_vma=False,
    )
```

```python
import numpy as np
import jax
import jax.numpy as jnp
from jax import lax
from jax.sharding import Mesh
from jax.sharding import PartitionSpec as P

PP = ("x", "yhi")
EP = ("z", "ylo", "core")
CHIPS = ("z", "ylo")
RING = ("x", "yhi", "ylo")


def ring_route(sections, distance):
    route = []
    for p in range(sections):
        for lo in range(2):
            route.append((p * 2 + lo, ((p + distance) % sections) * 2 + (1 - lo)))
    return route


def swap_ylo(block):
    return lax.ppermute(block, "ylo", [(0, 1), (1, 0)])


def slot_table(route_ids, expert_count, capacity):
    token_count, choice_count = route_ids.shape
    flattened = route_ids.reshape(token_count * choice_count)
    onehot = (flattened[:, None] == jnp.arange(expert_count, dtype=jnp.int32)[None, :]).astype(
        jnp.int32
    )
    earlier = jnp.cumsum(onehot, axis=0) - onehot
    slot_index = jnp.sum(earlier * onehot, axis=1)
    slot_match = (slot_index[:, None] == jnp.arange(capacity, dtype=jnp.int32)[None, :]).astype(
        jnp.float32
    )
    expert_match = onehot.astype(jnp.float32)
    joined = jnp.einsum("re,rc->rec", expert_match, slot_match).reshape(
        token_count, choice_count, expert_count, capacity
    )
    return jnp.transpose(jnp.sum(joined, axis=1), (1, 2, 0))


def swiglu_backward(upstream, saved):
    hid_units = upstream.shape[-1]
    pre_float = saved.astype(jnp.float32)
    gate_pre = pre_float[..., :hid_units]
    up_pre = pre_float[..., hid_units:]
    sigmoid_gate = jax.nn.sigmoid(gate_pre)
    upstream_float = upstream.astype(jnp.float32)
    grad_gate = upstream_float * up_pre * sigmoid_gate * (1.0 + gate_pre * (1.0 - sigmoid_gate))
    grad_up = upstream_float * gate_pre * sigmoid_gate
    return jnp.concatenate([grad_gate, grad_up], axis=-1).astype(jnp.bfloat16)


def make_shards(sections, zs):
    chips = 2 * zs

    def shards(prev_out, fwd_experts, expert_weights, bwd_experts, grad_hidden, saved_pre):
        experts = chips
        capacity = grad_hidden.shape[3]
        hid_units = grad_hidden.shape[4]
        model_width = prev_out.shape[2]
        weights = expert_weights[0, 0]
        core = lax.axis_index("core")
        chip = jnp.arange(chips, dtype=jnp.int32)
        worked = (chip // 2) * 4 + (1 - chip % 2) * 2

        ids = swap_ylo(jnp.concatenate([fwd_experts[0], bwd_experts[0]], axis=1))
        fwd_ids = ids[:, : fwd_experts.shape[2]]
        bwd_ids = ids[:, fwd_experts.shape[2] :]

        rows = lax.ppermute(prev_out[0], RING, ring_route(sections, 1))

        order = jnp.concatenate([worked + core, worked + 1 - core])
        upstream = jnp.take(grad_hidden[0, 0], order, axis=0)
        saved = jnp.take(saved_pre[0, 0], order, axis=0)
        grad_pre = swiglu_backward(upstream, saved).reshape(2, chips, capacity, 2 * hid_units)
        partial_rows = jnp.einsum(
            "kech,dh->kecd", grad_pre, weights, preferred_element_type=jnp.float32
        ).astype(jnp.bfloat16)
        other_part = lax.ppermute(partial_rows[1], "core", [(0, 1), (1, 0)])
        pair_sum = (partial_rows[0].astype(jnp.float32) + other_part.astype(jnp.float32)).astype(
            jnp.bfloat16
        )
        returned = lax.all_to_all(pair_sum, CHIPS, split_axis=0, concat_axis=0, tiled=True)
        rows, returned = lax.optimization_barrier((rows, returned))

        fwd_table = slot_table(fwd_ids, experts, capacity).astype(jnp.bfloat16)
        picked = jnp.einsum(
            "ect,td->ecd", fwd_table, rows, preferred_element_type=jnp.float32
        ).astype(jnp.bfloat16)
        bwd_table = slot_table(bwd_ids, experts, capacity).astype(jnp.bfloat16)
        grad_in = jnp.einsum(
            "ect,ecd->td", bwd_table, returned, preferred_element_type=jnp.float32
        ).astype(jnp.bfloat16)
        picked, grad_in = lax.optimization_barrier((picked, grad_in))
        grad_rows = lax.ppermute(grad_in, RING, ring_route(sections, -1))

        arrived = lax.all_to_all(picked, CHIPS, split_axis=0, concat_axis=0, tiled=True)

        both = lax.all_gather(arrived, "core", axis=0, tiled=False)
        projected = jnp.einsum(
            "scd,dh->sch",
            both.reshape(2 * experts, capacity, model_width),
            weights,
            preferred_element_type=jnp.float32,
        )
        hidden = (jax.nn.silu(projected[..., :hid_units]) * projected[..., hid_units:]).astype(
            jnp.bfloat16
        )
        blocks = np.arange(2 * experts)
        chip_of = (blocks // 4) * 2 + (1 - (blocks // 2) % 2)
        hidden = hidden[(blocks % 2) * chips + chip_of]
        return (hidden[None, None], grad_rows[None])

    return shards


def solution(mesh):
    sections = mesh.shape["pp"]
    groups = mesh.shape["ep"]
    zs = groups // 4
    devices = np.asarray(mesh.devices).reshape(sections // 2, 2, zs, 2, 2)
    fine = Mesh(devices, PP + EP)
    placed = (
        P(PP, EP, None),
        P(PP, EP, None),
        P(PP, EP, None, None),
        P(PP, EP, None),
        P(PP, EP, None, None, None),
        P(PP, EP, None, None, None),
    )
    return jax.shard_map(
        make_shards(sections, zs),
        mesh=fine,
        in_specs=placed,
        out_specs=(P(PP, EP, None, None, None), P(PP, EP, None)),
        check_vma=False,
    )
```

```python
import numpy as np
import jax
import jax.numpy as jnp
from jax import lax
from jax.sharding import Mesh
from jax.sharding import PartitionSpec as P

PP = ("x", "yhi")
EP = ("z", "ylo", "core")
CHIPS = ("z", "ylo")
RING = ("x", "yhi", "ylo")


def ring_route(sections, distance):
    route = []
    for p in range(sections):
        for lo in range(2):
            route.append((p * 2 + lo, ((p + distance) % sections) * 2 + (1 - lo)))
    return route


def swap_ylo(block):
    return lax.ppermute(block, "ylo", [(0, 1), (1, 0)])


def slot_table(route_ids, expert_count, capacity):
    token_count, choice_count = route_ids.shape
    flattened = route_ids.reshape(token_count * choice_count)
    onehot = (flattened[:, None] == jnp.arange(expert_count, dtype=jnp.int32)[None, :]).astype(
        jnp.int32
    )
    earlier = jnp.cumsum(onehot, axis=0) - onehot
    slot_index = jnp.sum(earlier * onehot, axis=1)
    slot_match = (slot_index[:, None] == jnp.arange(capacity, dtype=jnp.int32)[None, :]).astype(
        jnp.float32
    )
    expert_match = onehot.astype(jnp.float32)
    joined = jnp.einsum("re,rc->rec", expert_match, slot_match).reshape(
        token_count, choice_count, expert_count, capacity
    )
    return jnp.transpose(jnp.sum(joined, axis=1), (1, 2, 0))


def swiglu_backward(upstream, saved):
    hid_units = upstream.shape[-1]
    pre_float = saved.astype(jnp.float32)
    gate_pre = pre_float[..., :hid_units]
    up_pre = pre_float[..., hid_units:]
    sigmoid_gate = jax.nn.sigmoid(gate_pre)
    upstream_float = upstream.astype(jnp.float32)
    grad_gate = upstream_float * up_pre * sigmoid_gate * (1.0 + gate_pre * (1.0 - sigmoid_gate))
    grad_up = upstream_float * gate_pre * sigmoid_gate
    return jnp.concatenate([grad_gate, grad_up], axis=-1).astype(jnp.bfloat16)


def make_shards(sections, zs):
    chips = 2 * zs

    def shards(prev_out, fwd_experts, expert_weights, bwd_experts, grad_hidden, saved_pre):
        experts = chips
        capacity = grad_hidden.shape[3]
        hid_units = grad_hidden.shape[4]
        model_width = prev_out.shape[2]
        weights = expert_weights[0, 0]
        core = lax.axis_index("core")
        chip = jnp.arange(chips, dtype=jnp.int32)
        worked = (chip // 2) * 4 + (1 - chip % 2) * 2

        ids = swap_ylo(jnp.concatenate([fwd_experts[0], bwd_experts[0]], axis=1))
        fwd_ids = ids[:, : fwd_experts.shape[2]]
        bwd_ids = ids[:, fwd_experts.shape[2] :]

        rows = lax.ppermute(prev_out[0], RING, ring_route(sections, 1))

        order = jnp.concatenate([worked + core, worked + 1 - core])
        upstream = jnp.take(grad_hidden[0, 0], order, axis=0)
        saved = jnp.take(saved_pre[0, 0], order, axis=0)
        grad_pre = swiglu_backward(upstream, saved).reshape(2, chips, capacity, 2 * hid_units)
        send_part = jnp.einsum(
            "ech,dh->ecd", grad_pre[1], weights, preferred_element_type=jnp.float32
        ).astype(jnp.bfloat16)
        other_part = lax.ppermute(send_part, "core", [(0, 1), (1, 0)])
        keep_part = jnp.einsum(
            "ech,dh->ecd", grad_pre[0], weights, preferred_element_type=jnp.float32
        ).astype(jnp.bfloat16)
        pair_sum = (keep_part.astype(jnp.float32) + other_part.astype(jnp.float32)).astype(
            jnp.bfloat16
        )
        returned = lax.all_to_all(pair_sum, CHIPS, split_axis=0, concat_axis=0, tiled=True)
        rows, returned = lax.optimization_barrier((rows, returned))

        fwd_table = slot_table(fwd_ids, experts, capacity).astype(jnp.bfloat16)
        picked = jnp.einsum(
            "ect,td->ecd", fwd_table, rows, preferred_element_type=jnp.float32
        ).astype(jnp.bfloat16)
        bwd_table = slot_table(bwd_ids, experts, capacity).astype(jnp.bfloat16)
        grad_in = jnp.einsum(
            "ect,ecd->td", bwd_table, returned, preferred_element_type=jnp.float32
        ).astype(jnp.bfloat16)
        picked, grad_in = lax.optimization_barrier((picked, grad_in))
        grad_rows = lax.ppermute(grad_in, RING, ring_route(sections, -1))

        arrived = lax.all_to_all(picked, CHIPS, split_axis=0, concat_axis=0, tiled=True)

        partner = lax.ppermute(arrived, "core", [(0, 1), (1, 0)])
        own_proj = jnp.einsum("scd,dh->sch", arrived, weights, preferred_element_type=jnp.float32)
        partner_proj = jnp.einsum(
            "scd,dh->sch", partner, weights, preferred_element_type=jnp.float32
        )
        projected = jnp.where(
            core == 0,
            jnp.concatenate([own_proj, partner_proj]),
            jnp.concatenate([partner_proj, own_proj]),
        )
        hidden = (jax.nn.silu(projected[..., :hid_units]) * projected[..., hid_units:]).astype(
            jnp.bfloat16
        )
        blocks = np.arange(2 * experts)
        chip_of = (blocks // 4) * 2 + (1 - (blocks // 2) % 2)
        hidden = hidden[(blocks % 2) * chips + chip_of]
        return (hidden[None, None], grad_rows[None])

    return shards


def solution(mesh):
    sections = mesh.shape["pp"]
    groups = mesh.shape["ep"]
    zs = groups // 4
    devices = np.asarray(mesh.devices).reshape(sections // 2, 2, zs, 2, 2)
    fine = Mesh(devices, PP + EP)
    placed = (
        P(PP, EP, None),
        P(PP, EP, None),
        P(PP, EP, None, None),
        P(PP, EP, None),
        P(PP, EP, None, None, None),
        P(PP, EP, None, None, None),
    )
    return jax.shard_map(
        make_shards(sections, zs),
        mesh=fine,
        in_specs=placed,
        out_specs=(P(PP, EP, None, None, None), P(PP, EP, None)),
        check_vma=False,
    )
```

```python
import numpy as np
import jax
import jax.numpy as jnp
from jax import lax
from jax.sharding import Mesh
from jax.sharding import PartitionSpec as P

PP = ("x", "yhi")
EP = ("z", "ylo", "core")
CHIPS = ("z", "ylo")
RING = ("x", "yhi", "ylo")


def ring_route(sections, distance):
    route = []
    for p in range(sections):
        for lo in range(2):
            route.append((p * 2 + lo, ((p + distance) % sections) * 2 + (1 - lo)))
    return route


def swap_ylo(block):
    return lax.ppermute(block, "ylo", [(0, 1), (1, 0)])


def slot_table(route_ids, expert_count, capacity):
    token_count, choice_count = route_ids.shape
    flattened = route_ids.reshape(token_count * choice_count)
    onehot = (flattened[:, None] == jnp.arange(expert_count, dtype=jnp.int32)[None, :]).astype(
        jnp.int32
    )
    earlier = jnp.cumsum(onehot, axis=0) - onehot
    slot_index = jnp.sum(earlier * onehot, axis=1)
    slot_match = (slot_index[:, None] == jnp.arange(capacity, dtype=jnp.int32)[None, :]).astype(
        jnp.float32
    )
    expert_match = onehot.astype(jnp.float32)
    joined = jnp.einsum("re,rc->rec", expert_match, slot_match).reshape(
        token_count, choice_count, expert_count, capacity
    )
    return jnp.transpose(jnp.sum(joined, axis=1), (1, 2, 0))


def swiglu_backward(upstream, saved):
    hid_units = upstream.shape[-1]
    pre_float = saved.astype(jnp.float32)
    gate_pre = pre_float[..., :hid_units]
    up_pre = pre_float[..., hid_units:]
    sigmoid_gate = jax.nn.sigmoid(gate_pre)
    upstream_float = upstream.astype(jnp.float32)
    grad_gate = upstream_float * up_pre * sigmoid_gate * (1.0 + gate_pre * (1.0 - sigmoid_gate))
    grad_up = upstream_float * gate_pre * sigmoid_gate
    return jnp.concatenate([grad_gate, grad_up], axis=-1).astype(jnp.bfloat16)


def make_shards(sections, zs):
    chips = 2 * zs

    def shards(prev_out, fwd_experts, expert_weights, bwd_experts, grad_hidden, saved_pre):
        experts = chips
        capacity = grad_hidden.shape[3]
        hid_units = grad_hidden.shape[4]
        model_width = prev_out.shape[2]
        weights = expert_weights[0, 0]
        core = lax.axis_index("core")
        chip = jnp.arange(chips, dtype=jnp.int32)
        worked = (chip // 2) * 4 + (1 - chip % 2) * 2

        ids = swap_ylo(jnp.concatenate([fwd_experts[0], bwd_experts[0]], axis=1))
        fwd_ids = ids[:, : fwd_experts.shape[2]]
        bwd_ids = ids[:, fwd_experts.shape[2] :]

        rows = lax.ppermute(prev_out[0], RING, ring_route(sections, 1))

        order = jnp.concatenate([worked + core, worked + 1 - core])
        upstream = jnp.take(grad_hidden[0, 0], order, axis=0)
        saved = jnp.take(saved_pre[0, 0], order, axis=0)
        grad_pre = swiglu_backward(upstream, saved).reshape(2, chips, capacity, 2 * hid_units)
        partial_rows = jnp.einsum(
            "kech,dh->kecd", grad_pre, weights, preferred_element_type=jnp.float32
        ).astype(jnp.bfloat16)
        other_part = lax.ppermute(partial_rows[1], "core", [(0, 1), (1, 0)])
        pair_sum = (partial_rows[0].astype(jnp.float32) + other_part.astype(jnp.float32)).astype(
            jnp.bfloat16
        )
        returned = lax.all_to_all(pair_sum, CHIPS, split_axis=0, concat_axis=0, tiled=True)
        rows, returned = lax.optimization_barrier((rows, returned))

        fwd_table = slot_table(fwd_ids, experts, capacity).astype(jnp.bfloat16)
        picked = jnp.einsum(
            "ect,td->ecd", fwd_table, rows, preferred_element_type=jnp.float32
        ).astype(jnp.bfloat16)
        bwd_table = slot_table(bwd_ids, experts, capacity).astype(jnp.bfloat16)
        grad_in = jnp.einsum(
            "ect,ecd->td", bwd_table, returned, preferred_element_type=jnp.float32
        ).astype(jnp.bfloat16)
        picked, grad_in = lax.optimization_barrier((picked, grad_in))
        grad_rows = lax.ppermute(grad_in, RING, ring_route(sections, -1))

        arrived = lax.all_to_all(picked, CHIPS, split_axis=0, concat_axis=0, tiled=True)

        both = lax.all_gather(arrived, "core", axis=0, tiled=False)
        projected = jnp.einsum(
            "scd,dh->sch",
            both.reshape(2 * experts, capacity, model_width),
            weights,
            preferred_element_type=jnp.float32,
        )
        hidden = (jax.nn.silu(projected[..., :hid_units]) * projected[..., hid_units:]).astype(
            jnp.bfloat16
        )
        blocks = np.arange(2 * experts)
        chip_of = (blocks // 4) * 2 + (1 - (blocks // 2) % 2)
        hidden = hidden[(blocks % 2) * chips + chip_of]
        hidden, grad_rows = lax.optimization_barrier((hidden, grad_rows))
        return (hidden[None, None], grad_rows[None])

    return shards


def solution(mesh):
    sections = mesh.shape["pp"]
    groups = mesh.shape["ep"]
    zs = groups // 4
    devices = np.asarray(mesh.devices).reshape(sections // 2, 2, zs, 2, 2)
    fine = Mesh(devices, PP + EP)
    placed = (
        P(PP, EP, None),
        P(PP, EP, None),
        P(PP, EP, None, None),
        P(PP, EP, None),
        P(PP, EP, None, None, None),
        P(PP, EP, None, None, None),
    )
    return jax.shard_map(
        make_shards(sections, zs),
        mesh=fine,
        in_specs=placed,
        out_specs=(P(PP, EP, None, None, None), P(PP, EP, None)),
        check_vma=False,
    )
```

```python
import numpy as np
import jax
import jax.numpy as jnp
from jax import lax
from jax.sharding import Mesh
from jax.sharding import PartitionSpec as P

PP = ("x", "yhi")
EP = ("z", "ylo", "core")
CHIPS = ("z", "ylo")
RING = ("x", "yhi", "ylo")


def ring_route(sections, distance):
    route = []
    for p in range(sections):
        for lo in range(2):
            route.append((p * 2 + lo, ((p + distance) % sections) * 2 + (1 - lo)))
    return route


def swap_ylo(block):
    return lax.ppermute(block, "ylo", [(0, 1), (1, 0)])


def slot_table(route_ids, expert_count, capacity):
    token_count, choice_count = route_ids.shape
    flattened = route_ids.reshape(token_count * choice_count)
    onehot = (flattened[:, None] == jnp.arange(expert_count, dtype=jnp.int32)[None, :]).astype(
        jnp.int32
    )
    earlier = jnp.cumsum(onehot, axis=0) - onehot
    slot_index = jnp.sum(earlier * onehot, axis=1)
    slot_match = (slot_index[:, None] == jnp.arange(capacity, dtype=jnp.int32)[None, :]).astype(
        jnp.float32
    )
    expert_match = onehot.astype(jnp.float32)
    joined = jnp.einsum("re,rc->rec", expert_match, slot_match).reshape(
        token_count, choice_count, expert_count, capacity
    )
    return jnp.transpose(jnp.sum(joined, axis=1), (1, 2, 0))


def swiglu_backward(upstream, saved):
    hid_units = upstream.shape[-1]
    pre_float = saved.astype(jnp.float32)
    gate_pre = pre_float[..., :hid_units]
    up_pre = pre_float[..., hid_units:]
    sigmoid_gate = jax.nn.sigmoid(gate_pre)
    upstream_float = upstream.astype(jnp.float32)
    grad_gate = upstream_float * up_pre * sigmoid_gate * (1.0 + gate_pre * (1.0 - sigmoid_gate))
    grad_up = upstream_float * gate_pre * sigmoid_gate
    return jnp.concatenate([grad_gate, grad_up], axis=-1).astype(jnp.bfloat16)


def make_shards(sections, zs):
    chips = 2 * zs

    def shards(prev_out, fwd_experts, expert_weights, bwd_experts, grad_hidden, saved_pre):
        experts = chips
        capacity = grad_hidden.shape[3]
        hid_units = grad_hidden.shape[4]
        model_width = prev_out.shape[2]
        weights = expert_weights[0, 0]
        core = lax.axis_index("core")
        chip = jnp.arange(chips, dtype=jnp.int32)
        worked = (chip // 2) * 4 + (1 - chip % 2) * 2

        ids = swap_ylo(jnp.concatenate([fwd_experts[0], bwd_experts[0]], axis=1))
        fwd_ids = ids[:, : fwd_experts.shape[2]]
        bwd_ids = ids[:, fwd_experts.shape[2] :]

        rows = lax.ppermute(prev_out[0], RING, ring_route(sections, 1))

        order = jnp.concatenate([worked, worked + 1])
        upstream = jnp.take(grad_hidden[0, 0], order, axis=0)
        saved = jnp.take(saved_pre[0, 0], order, axis=0)
        grad_pre = swiglu_backward(upstream, saved).reshape(2, chips, capacity, 2 * hid_units)
        partial_rows = jnp.einsum(
            "kech,dh->kecd", grad_pre, weights, preferred_element_type=jnp.float32
        ).astype(jnp.bfloat16)
        pair_sum = lax.psum_scatter(partial_rows, "core", scatter_dimension=0, tiled=False)
        returned = lax.all_to_all(pair_sum, CHIPS, split_axis=0, concat_axis=0, tiled=True)
        rows, returned = lax.optimization_barrier((rows, returned))

        fwd_table = slot_table(fwd_ids, experts, capacity).astype(jnp.bfloat16)
        picked = jnp.einsum(
            "ect,td->ecd", fwd_table, rows, preferred_element_type=jnp.float32
        ).astype(jnp.bfloat16)
        bwd_table = slot_table(bwd_ids, experts, capacity).astype(jnp.bfloat16)
        grad_in = jnp.einsum(
            "ect,ecd->td", bwd_table, returned, preferred_element_type=jnp.float32
        ).astype(jnp.bfloat16)
        picked, grad_in = lax.optimization_barrier((picked, grad_in))
        grad_rows = lax.ppermute(grad_in, RING, ring_route(sections, -1))

        arrived = lax.all_to_all(picked, CHIPS, split_axis=0, concat_axis=0, tiled=True)

        both = lax.all_gather(arrived, "core", axis=0, tiled=False)
        projected = jnp.einsum(
            "scd,dh->sch",
            both.reshape(2 * experts, capacity, model_width),
            weights,
            preferred_element_type=jnp.float32,
        )
        hidden = (jax.nn.silu(projected[..., :hid_units]) * projected[..., hid_units:]).astype(
            jnp.bfloat16
        )
        blocks = np.arange(2 * experts)
        chip_of = (blocks // 4) * 2 + (1 - (blocks // 2) % 2)
        hidden = hidden[(blocks % 2) * chips + chip_of]
        hidden, grad_rows = lax.optimization_barrier((hidden, grad_rows))
        return (hidden[None, None], grad_rows[None])

    return shards


def solution(mesh):
    sections = mesh.shape["pp"]
    groups = mesh.shape["ep"]
    zs = groups // 4
    devices = np.asarray(mesh.devices).reshape(sections // 2, 2, zs, 2, 2)
    fine = Mesh(devices, PP + EP)
    placed = (
        P(PP, EP, None),
        P(PP, EP, None),
        P(PP, EP, None, None),
        P(PP, EP, None),
        P(PP, EP, None, None, None),
        P(PP, EP, None, None, None),
    )
    return jax.shard_map(
        make_shards(sections, zs),
        mesh=fine,
        in_specs=placed,
        out_specs=(P(PP, EP, None, None, None), P(PP, EP, None)),
        check_vma=False,
    )
```

```python
import numpy as np
import jax
import jax.numpy as jnp
from jax import lax
from jax.sharding import Mesh
from jax.sharding import PartitionSpec as P

PP = ("x", "yhi")
EP = ("z", "ylo", "core")
CHIPS = ("z", "ylo")
RING = ("x", "yhi", "ylo")


def ring_route(sections, distance):
    route = []
    for p in range(sections):
        for lo in range(2):
            route.append((p * 2 + lo, ((p + distance) % sections) * 2 + (1 - lo)))
    return route


def swap_ylo(block):
    return lax.ppermute(block, "ylo", [(0, 1), (1, 0)])


def slot_table(route_ids, expert_count, capacity):
    token_count, choice_count = route_ids.shape
    flattened = route_ids.reshape(token_count * choice_count)
    onehot = (flattened[:, None] == jnp.arange(expert_count, dtype=jnp.int32)[None, :]).astype(
        jnp.int32
    )
    earlier = jnp.cumsum(onehot, axis=0) - onehot
    slot_index = jnp.sum(earlier * onehot, axis=1)
    slot_match = (slot_index[:, None] == jnp.arange(capacity, dtype=jnp.int32)[None, :]).astype(
        jnp.float32
    )
    expert_match = onehot.astype(jnp.float32)
    joined = jnp.einsum("re,rc->rec", expert_match, slot_match).reshape(
        token_count, choice_count, expert_count, capacity
    )
    return jnp.transpose(jnp.sum(joined, axis=1), (1, 2, 0))


def swiglu_backward(upstream, saved):
    hid_units = upstream.shape[-1]
    pre_float = saved.astype(jnp.float32)
    gate_pre = pre_float[..., :hid_units]
    up_pre = pre_float[..., hid_units:]
    sigmoid_gate = jax.nn.sigmoid(gate_pre)
    upstream_float = upstream.astype(jnp.float32)
    grad_gate = upstream_float * up_pre * sigmoid_gate * (1.0 + gate_pre * (1.0 - sigmoid_gate))
    grad_up = upstream_float * gate_pre * sigmoid_gate
    return jnp.concatenate([grad_gate, grad_up], axis=-1).astype(jnp.bfloat16)


def make_shards(sections, zs):
    chips = 2 * zs

    def shards(prev_out, fwd_experts, expert_weights, bwd_experts, grad_hidden, saved_pre):
        experts = chips
        capacity = grad_hidden.shape[3]
        hid_units = grad_hidden.shape[4]
        model_width = prev_out.shape[2]
        weights = expert_weights[0, 0]
        core = lax.axis_index("core")
        chip = jnp.arange(chips, dtype=jnp.int32)
        worked = (chip // 2) * 4 + (1 - chip % 2) * 2

        ids = swap_ylo(jnp.concatenate([fwd_experts[0], bwd_experts[0]], axis=1))
        fwd_ids = ids[:, : fwd_experts.shape[2]]
        bwd_ids = ids[:, fwd_experts.shape[2] :]

        rows = lax.ppermute(prev_out[0], RING, ring_route(sections, 1))

        fwd_table = slot_table(fwd_ids, experts, capacity).astype(jnp.bfloat16)
        picked = jnp.einsum(
            "ect,td->ecd", fwd_table, rows, preferred_element_type=jnp.float32
        ).astype(jnp.bfloat16)
        arrived = lax.all_to_all(picked, CHIPS, split_axis=0, concat_axis=0, tiled=True)
        picked, order_in = lax.optimization_barrier((picked, jnp.arange(2 * chips, dtype=jnp.int32)))
        order = jnp.concatenate([worked + core, worked + 1 - core]) + 0 * order_in
        upstream = jnp.take(grad_hidden[0, 0], order, axis=0)
        saved = jnp.take(saved_pre[0, 0], order, axis=0)
        grad_pre = swiglu_backward(upstream, saved).reshape(2, chips, capacity, 2 * hid_units)
        partial_rows = jnp.einsum(
            "kech,dh->kecd", grad_pre, weights, preferred_element_type=jnp.float32
        ).astype(jnp.bfloat16)
        other_part = lax.ppermute(partial_rows[1], "core", [(0, 1), (1, 0)])
        pair_sum = (partial_rows[0].astype(jnp.float32) + other_part.astype(jnp.float32)).astype(
            jnp.bfloat16
        )
        returned = lax.all_to_all(pair_sum, CHIPS, split_axis=0, concat_axis=0, tiled=True)

        bwd_table = slot_table(bwd_ids, experts, capacity).astype(jnp.bfloat16)
        grad_in = jnp.einsum(
            "ect,ecd->td", bwd_table, returned, preferred_element_type=jnp.float32
        ).astype(jnp.bfloat16)
        grad_rows = lax.ppermute(grad_in, RING, ring_route(sections, -1))


        both = lax.all_gather(arrived, "core", axis=0, tiled=False)
        projected = jnp.einsum(
            "scd,dh->sch",
            both.reshape(2 * experts, capacity, model_width),
            weights,
            preferred_element_type=jnp.float32,
        )
        hidden = (jax.nn.silu(projected[..., :hid_units]) * projected[..., hid_units:]).astype(
            jnp.bfloat16
        )
        blocks = np.arange(2 * experts)
        chip_of = (blocks // 4) * 2 + (1 - (blocks // 2) % 2)
        hidden = hidden[(blocks % 2) * chips + chip_of]
        hidden, grad_rows = lax.optimization_barrier((hidden, grad_rows))
        return (hidden[None, None], grad_rows[None])

    return shards


def solution(mesh):
    sections = mesh.shape["pp"]
    groups = mesh.shape["ep"]
    zs = groups // 4
    devices = np.asarray(mesh.devices).reshape(sections // 2, 2, zs, 2, 2)
    fine = Mesh(devices, PP + EP)
    placed = (
        P(PP, EP, None),
        P(PP, EP, None),
        P(PP, EP, None, None),
        P(PP, EP, None),
        P(PP, EP, None, None, None),
        P(PP, EP, None, None, None),
    )
    return jax.shard_map(
        make_shards(sections, zs),
        mesh=fine,
        in_specs=placed,
        out_specs=(P(PP, EP, None, None, None), P(PP, EP, None)),
        check_vma=False,
    )
```

```python
import numpy as np
import jax
import jax.numpy as jnp
from jax import lax
from jax.sharding import Mesh
from jax.sharding import PartitionSpec as P

PP = ("x", "yhi")
EP = ("z", "ylo", "core")
CHIPS = ("z", "ylo")
RING = ("x", "yhi", "ylo")


def ring_route(sections, distance):
    route = []
    for p in range(sections):
        for lo in range(2):
            route.append((p * 2 + lo, ((p + distance) % sections) * 2 + (1 - lo)))
    return route


def swap_ylo(block):
    return lax.ppermute(block, "ylo", [(0, 1), (1, 0)])


def slot_table(route_ids, expert_count, capacity):
    token_count, choice_count = route_ids.shape
    flattened = route_ids.reshape(token_count * choice_count)
    onehot = (flattened[:, None] == jnp.arange(expert_count, dtype=jnp.int32)[None, :]).astype(
        jnp.int32
    )
    earlier = jnp.cumsum(onehot, axis=0) - onehot
    slot_index = jnp.sum(earlier * onehot, axis=1)
    slot_match = (slot_index[:, None] == jnp.arange(capacity, dtype=jnp.int32)[None, :]).astype(
        jnp.float32
    )
    expert_match = onehot.astype(jnp.float32)
    joined = jnp.einsum("re,rc->rec", expert_match, slot_match).reshape(
        token_count, choice_count, expert_count, capacity
    )
    return jnp.transpose(jnp.sum(joined, axis=1), (1, 2, 0))


def swiglu_backward(upstream, saved):
    hid_units = upstream.shape[-1]
    pre_float = saved.astype(jnp.float32)
    gate_pre = pre_float[..., :hid_units]
    up_pre = pre_float[..., hid_units:]
    sigmoid_gate = jax.nn.sigmoid(gate_pre)
    upstream_float = upstream.astype(jnp.float32)
    grad_gate = upstream_float * up_pre * sigmoid_gate * (1.0 + gate_pre * (1.0 - sigmoid_gate))
    grad_up = upstream_float * gate_pre * sigmoid_gate
    return jnp.concatenate([grad_gate, grad_up], axis=-1).astype(jnp.bfloat16)


def make_shards(sections, zs):
    chips = 2 * zs

    def shards(prev_out, fwd_experts, expert_weights, bwd_experts, grad_hidden, saved_pre):
        experts = chips
        capacity = grad_hidden.shape[3]
        hid_units = grad_hidden.shape[4]
        model_width = prev_out.shape[2]
        weights = expert_weights[0, 0]
        core = lax.axis_index("core")
        chip = jnp.arange(chips, dtype=jnp.int32)
        worked = (chip // 2) * 4 + (1 - chip % 2) * 2

        ids = swap_ylo(jnp.concatenate([fwd_experts[0], bwd_experts[0]], axis=1))
        fwd_ids = ids[:, : fwd_experts.shape[2]]
        bwd_ids = ids[:, fwd_experts.shape[2] :]

        rows = lax.ppermute(prev_out[0], RING, ring_route(sections, 1))

        order = jnp.concatenate([worked + core, worked + 1 - core])
        upstream = jnp.take(grad_hidden[0, 0], order, axis=0)
        saved = jnp.take(saved_pre[0, 0], order, axis=0)
        grad_pre = swiglu_backward(upstream, saved).reshape(2, chips, capacity, 2 * hid_units)
        partial_rows = jnp.einsum(
            "kech,dh->kecd", grad_pre, weights, preferred_element_type=jnp.float32
        ).astype(jnp.bfloat16)
        other_part = lax.ppermute(partial_rows[1], "core", [(0, 1), (1, 0)])
        pair_sum = (partial_rows[0].astype(jnp.float32) + other_part.astype(jnp.float32)).astype(
            jnp.bfloat16
        )
        returned = lax.all_to_all(pair_sum, CHIPS, split_axis=0, concat_axis=0, tiled=True)
        rows, returned = lax.optimization_barrier((rows, returned))

        fwd_table = slot_table(fwd_ids, experts, capacity).astype(jnp.bfloat16)
        picked = jnp.einsum(
            "ect,td->ecd", fwd_table, rows, preferred_element_type=jnp.float32
        ).astype(jnp.bfloat16)
        arrived = lax.all_to_all(picked, CHIPS, split_axis=0, concat_axis=0, tiled=True)

        partner = lax.ppermute(arrived, "core", [(0, 1), (1, 0)])
        bwd_table = slot_table(bwd_ids, experts, capacity).astype(jnp.bfloat16)
        grad_in = jnp.einsum(
            "ect,ecd->td", bwd_table, returned, preferred_element_type=jnp.float32
        ).astype(jnp.bfloat16)
        grad_in, partner = lax.optimization_barrier((grad_in, partner))
        grad_rows = lax.ppermute(grad_in, RING, ring_route(sections, -1))

        projected = jnp.einsum(
            "scd,dh->sch",
            jnp.concatenate([arrived, partner]),
            weights,
            preferred_element_type=jnp.float32,
        )
        hidden = (jax.nn.silu(projected[..., :hid_units]) * projected[..., hid_units:]).astype(
            jnp.bfloat16
        )
        blocks = jnp.arange(2 * experts, dtype=jnp.int32)
        chip_of = (blocks // 4) * 2 + (1 - (blocks // 2) % 2)
        hidden = jnp.take(hidden, jnp.where(blocks % 2 == core, chip_of, chips + chip_of), axis=0)
        hidden, grad_rows = lax.optimization_barrier((hidden, grad_rows))
        return (hidden[None, None], grad_rows[None])

    return shards


def solution(mesh):
    sections = mesh.shape["pp"]
    groups = mesh.shape["ep"]
    zs = groups // 4
    devices = np.asarray(mesh.devices).reshape(sections // 2, 2, zs, 2, 2)
    fine = Mesh(devices, PP + EP)
    placed = (
        P(PP, EP, None),
        P(PP, EP, None),
        P(PP, EP, None, None),
        P(PP, EP, None),
        P(PP, EP, None, None, None),
        P(PP, EP, None, None, None),
    )
    return jax.shard_map(
        make_shards(sections, zs),
        mesh=fine,
        in_specs=placed,
        out_specs=(P(PP, EP, None, None, None), P(PP, EP, None)),
        check_vma=False,
    )
```

```python
import numpy as np
import jax
import jax.numpy as jnp
from jax import lax
from jax.sharding import Mesh
from jax.sharding import PartitionSpec as P

PP = ("x", "yhi")
EP = ("z", "ylo", "core")
CHIPS = ("z", "ylo")
RING = ("x", "yhi", "ylo")


def ring_route(sections, distance):
    route = []
    for p in range(sections):
        for lo in range(2):
            route.append((p * 2 + lo, ((p + distance) % sections) * 2 + (1 - lo)))
    return route


def swap_ylo(block):
    return lax.ppermute(block, "ylo", [(0, 1), (1, 0)])


def slot_table(route_ids, expert_count, capacity):
    token_count, choice_count = route_ids.shape
    flattened = route_ids.reshape(token_count * choice_count)
    onehot = (flattened[:, None] == jnp.arange(expert_count, dtype=jnp.int32)[None, :]).astype(
        jnp.int32
    )
    earlier = jnp.cumsum(onehot, axis=0) - onehot
    slot_index = jnp.sum(earlier * onehot, axis=1)
    slot_match = (slot_index[:, None] == jnp.arange(capacity, dtype=jnp.int32)[None, :]).astype(
        jnp.float32
    )
    expert_match = onehot.astype(jnp.float32)
    joined = jnp.einsum("re,rc->rec", expert_match, slot_match).reshape(
        token_count, choice_count, expert_count, capacity
    )
    return jnp.transpose(jnp.sum(joined, axis=1), (1, 2, 0))


def swiglu_backward(upstream, saved):
    hid_units = upstream.shape[-1]
    pre_float = saved.astype(jnp.float32)
    gate_pre = pre_float[..., :hid_units]
    up_pre = pre_float[..., hid_units:]
    sigmoid_gate = jax.nn.sigmoid(gate_pre)
    upstream_float = upstream.astype(jnp.float32)
    grad_gate = upstream_float * up_pre * sigmoid_gate * (1.0 + gate_pre * (1.0 - sigmoid_gate))
    grad_up = upstream_float * gate_pre * sigmoid_gate
    return jnp.concatenate([grad_gate, grad_up], axis=-1).astype(jnp.bfloat16)


def make_shards(sections, zs):
    chips = 2 * zs

    def shards(prev_out, fwd_experts, expert_weights, bwd_experts, grad_hidden, saved_pre):
        experts = chips
        capacity = grad_hidden.shape[3]
        hid_units = grad_hidden.shape[4]
        model_width = prev_out.shape[2]
        weights = expert_weights[0, 0]
        core = lax.axis_index("core")
        chip = jnp.arange(chips, dtype=jnp.int32)
        worked = (chip // 2) * 4 + (1 - chip % 2) * 2

        ids = swap_ylo(jnp.concatenate([fwd_experts[0], bwd_experts[0]], axis=1))
        fwd_ids = ids[:, : fwd_experts.shape[2]]
        bwd_ids = ids[:, fwd_experts.shape[2] :]

        rows = lax.ppermute(prev_out[0], RING, ring_route(sections, 1))

        def by_chip(blocks):
            split = blocks.reshape((zs, 2, 2) + blocks.shape[1:])[:, ::-1]
            return jnp.swapaxes(jnp.swapaxes(split, 1, 2), 0, 1).reshape(blocks.shape)

        grad_pre = swiglu_backward(by_chip(grad_hidden[0, 0]), by_chip(saved_pre[0, 0]))
        partial_rows = jnp.einsum(
            "kch,dh->kcd",
            grad_pre.reshape(2, chips * capacity, 2 * hid_units),
            weights,
            preferred_element_type=jnp.float32,
        ).astype(jnp.bfloat16).reshape(2, chips, capacity, model_width)
        send_part = lax.dynamic_index_in_dim(partial_rows, 1 - core, axis=0, keepdims=False)
        keep_part = lax.dynamic_index_in_dim(partial_rows, core, axis=0, keepdims=False)
        other_part = lax.ppermute(send_part, "core", [(0, 1), (1, 0)])
        pair_sum = (keep_part.astype(jnp.float32) + other_part.astype(jnp.float32)).astype(
            jnp.bfloat16
        )
        returned = lax.all_to_all(pair_sum, CHIPS, split_axis=0, concat_axis=0, tiled=True)
        rows, returned = lax.optimization_barrier((rows, returned))

        fwd_table = slot_table(fwd_ids, experts, capacity).astype(jnp.bfloat16)
        picked = jnp.einsum(
            "ect,td->ecd", fwd_table, rows, preferred_element_type=jnp.float32
        ).astype(jnp.bfloat16)
        arrived = lax.all_to_all(picked, CHIPS, split_axis=0, concat_axis=0, tiled=True)

        partner = lax.ppermute(arrived, "core", [(0, 1), (1, 0)])
        bwd_table = slot_table(bwd_ids, experts, capacity).astype(jnp.bfloat16)
        grad_in = jnp.einsum(
            "ect,ecd->td", bwd_table, returned, preferred_element_type=jnp.float32
        ).astype(jnp.bfloat16)
        grad_in, partner = lax.optimization_barrier((grad_in, partner))
        grad_rows = lax.ppermute(grad_in, RING, ring_route(sections, -1))

        projected = jnp.einsum(
            "scd,dh->sch",
            jnp.concatenate([arrived, partner]),
            weights,
            preferred_element_type=jnp.float32,
        )
        hidden = (jax.nn.silu(projected[..., :hid_units]) * projected[..., hid_units:]).astype(
            jnp.bfloat16
        )
        blocks = jnp.arange(2 * experts, dtype=jnp.int32)
        chip_of = (blocks // 4) * 2 + (1 - (blocks // 2) % 2)
        hidden = jnp.take(hidden, jnp.where(blocks % 2 == core, chip_of, chips + chip_of), axis=0)
        hidden, grad_rows = lax.optimization_barrier((hidden, grad_rows))
        return (hidden[None, None], grad_rows[None])

    return shards


def solution(mesh):
    sections = mesh.shape["pp"]
    groups = mesh.shape["ep"]
    zs = groups // 4
    devices = np.asarray(mesh.devices).reshape(sections // 2, 2, zs, 2, 2)
    fine = Mesh(devices, PP + EP)
    placed = (
        P(PP, EP, None),
        P(PP, EP, None),
        P(PP, EP, None, None),
        P(PP, EP, None),
        P(PP, EP, None, None, None),
        P(PP, EP, None, None, None),
    )
    return jax.shard_map(
        make_shards(sections, zs),
        mesh=fine,
        in_specs=placed,
        out_specs=(P(PP, EP, None, None, None), P(PP, EP, None)),
        check_vma=False,
    )
```

```python
import numpy as np
import jax
import jax.numpy as jnp
from jax import lax
from jax.sharding import Mesh
from jax.sharding import PartitionSpec as P

PP = ("x", "yhi")
EP = ("z", "ylo", "core")
CHIPS = ("z", "ylo")
RING = ("x", "yhi", "ylo")


def ring_route(sections, distance):
    route = []
    for p in range(sections):
        for lo in range(2):
            route.append((p * 2 + lo, ((p + distance) % sections) * 2 + (1 - lo)))
    return route


def swap_ylo(block):
    return lax.ppermute(block, "ylo", [(0, 1), (1, 0)])


def slot_table(route_ids, expert_count, capacity):
    token_count, choice_count = route_ids.shape
    flattened = route_ids.reshape(token_count * choice_count)
    onehot = (flattened[:, None] == jnp.arange(expert_count, dtype=jnp.int32)[None, :]).astype(
        jnp.int32
    )
    earlier = jnp.cumsum(onehot, axis=0) - onehot
    slot_index = jnp.sum(earlier * onehot, axis=1)
    slot_match = (slot_index[:, None] == jnp.arange(capacity, dtype=jnp.int32)[None, :]).astype(
        jnp.float32
    )
    expert_match = onehot.astype(jnp.float32)
    joined = jnp.einsum("re,rc->rec", expert_match, slot_match).reshape(
        token_count, choice_count, expert_count, capacity
    )
    return jnp.transpose(jnp.sum(joined, axis=1), (1, 2, 0))


def swiglu_backward(upstream, saved):
    hid_units = upstream.shape[-1]
    pre_float = saved.astype(jnp.float32)
    gate_pre = pre_float[..., :hid_units]
    up_pre = pre_float[..., hid_units:]
    sigmoid_gate = jax.nn.sigmoid(gate_pre)
    upstream_float = upstream.astype(jnp.float32)
    grad_gate = upstream_float * up_pre * sigmoid_gate * (1.0 + gate_pre * (1.0 - sigmoid_gate))
    grad_up = upstream_float * gate_pre * sigmoid_gate
    return jnp.concatenate([grad_gate, grad_up], axis=-1).astype(jnp.bfloat16)


def make_shards(sections, zs):
    chips = 2 * zs

    def shards(prev_out, fwd_experts, expert_weights, bwd_experts, grad_hidden, saved_pre):
        experts = chips
        capacity = grad_hidden.shape[3]
        hid_units = grad_hidden.shape[4]
        model_width = prev_out.shape[2]
        weights = expert_weights[0, 0]
        core = lax.axis_index("core")
        chip = jnp.arange(chips, dtype=jnp.int32)
        worked = (chip // 2) * 4 + (1 - chip % 2) * 2

        ids = swap_ylo(jnp.concatenate([fwd_experts[0], bwd_experts[0]], axis=1))
        fwd_ids = ids[:, : fwd_experts.shape[2]]
        bwd_ids = ids[:, fwd_experts.shape[2] :]

        rows = lax.ppermute(prev_out[0], RING, ring_route(sections, 1))

        order = jnp.concatenate([worked + core, worked + 1 - core])
        upstream = jnp.take(grad_hidden[0, 0], order, axis=0)
        saved = jnp.take(saved_pre[0, 0], order, axis=0)
        grad_pre = swiglu_backward(upstream, saved).reshape(2, chips, capacity, 2 * hid_units)
        width = model_width // 2
        sums = []
        for cols in (weights[:width], weights[width:]):
            part = jnp.einsum(
                "kech,dh->kecd", grad_pre, cols, preferred_element_type=jnp.float32
            ).astype(jnp.bfloat16)
            other = lax.ppermute(part[1], "core", [(0, 1), (1, 0)])
            sums.append(part[0].astype(jnp.float32) + other.astype(jnp.float32))
        pair_sum = jnp.concatenate(sums, axis=-1).astype(jnp.bfloat16)
        returned = lax.all_to_all(pair_sum, CHIPS, split_axis=0, concat_axis=0, tiled=True)
        rows, returned = lax.optimization_barrier((rows, returned))

        fwd_table = slot_table(fwd_ids, experts, capacity).astype(jnp.bfloat16)
        picked = jnp.einsum(
            "ect,td->ecd", fwd_table, rows, preferred_element_type=jnp.float32
        ).astype(jnp.bfloat16)
        arrived = lax.all_to_all(picked, CHIPS, split_axis=0, concat_axis=0, tiled=True)

        partner = lax.ppermute(arrived, "core", [(0, 1), (1, 0)])
        bwd_table = slot_table(bwd_ids, experts, capacity).astype(jnp.bfloat16)
        grad_in = jnp.einsum(
            "ect,ecd->td", bwd_table, returned, preferred_element_type=jnp.float32
        ).astype(jnp.bfloat16)
        grad_in, partner = lax.optimization_barrier((grad_in, partner))
        grad_rows = lax.ppermute(grad_in, RING, ring_route(sections, -1))

        projected = jnp.einsum(
            "scd,dh->sch",
            jnp.concatenate([arrived, partner]),
            weights,
            preferred_element_type=jnp.float32,
        )
        hidden = (jax.nn.silu(projected[..., :hid_units]) * projected[..., hid_units:]).astype(
            jnp.bfloat16
        )
        blocks = jnp.arange(2 * experts, dtype=jnp.int32)
        chip_of = (blocks // 4) * 2 + (1 - (blocks // 2) % 2)
        hidden = jnp.take(hidden, jnp.where(blocks % 2 == core, chip_of, chips + chip_of), axis=0)
        hidden, grad_rows = lax.optimization_barrier((hidden, grad_rows))
        return (hidden[None, None], grad_rows[None])

    return shards


def solution(mesh):
    sections = mesh.shape["pp"]
    groups = mesh.shape["ep"]
    zs = groups // 4
    devices = np.asarray(mesh.devices).reshape(sections // 2, 2, zs, 2, 2)
    fine = Mesh(devices, PP + EP)
    placed = (
        P(PP, EP, None),
        P(PP, EP, None),
        P(PP, EP, None, None),
        P(PP, EP, None),
        P(PP, EP, None, None, None),
        P(PP, EP, None, None, None),
    )
    return jax.shard_map(
        make_shards(sections, zs),
        mesh=fine,
        in_specs=placed,
        out_specs=(P(PP, EP, None, None, None), P(PP, EP, None)),
        check_vma=False,
    )
```

```python
import numpy as np
import jax
import jax.numpy as jnp
from jax import lax
from jax.sharding import Mesh
from jax.sharding import PartitionSpec as P

PP = ("x", "yhi")
EP = ("z", "ylo", "core")
CHIPS = ("z", "ylo")
RING = ("x", "yhi", "ylo")


def ring_route(sections, distance):
    route = []
    for p in range(sections):
        for lo in range(2):
            route.append((p * 2 + lo, ((p + distance) % sections) * 2 + (1 - lo)))
    return route


def swap_ylo(block):
    return lax.ppermute(block, "ylo", [(0, 1), (1, 0)])


def slot_table(route_ids, expert_count, capacity):
    token_count, choice_count = route_ids.shape
    flattened = route_ids.reshape(token_count * choice_count)
    onehot = (flattened[:, None] == jnp.arange(expert_count, dtype=jnp.int32)[None, :]).astype(
        jnp.int32
    )
    earlier = jnp.cumsum(onehot, axis=0) - onehot
    slot_index = jnp.sum(earlier * onehot, axis=1)
    slot_match = (slot_index[:, None] == jnp.arange(capacity, dtype=jnp.int32)[None, :]).astype(
        jnp.float32
    )
    expert_match = onehot.astype(jnp.float32)
    joined = jnp.einsum("re,rc->rec", expert_match, slot_match).reshape(
        token_count, choice_count, expert_count, capacity
    )
    return jnp.transpose(jnp.sum(joined, axis=1), (1, 2, 0))


def swiglu_backward(upstream, saved):
    hid_units = upstream.shape[-1]
    pre_float = saved.astype(jnp.float32)
    gate_pre = pre_float[..., :hid_units]
    up_pre = pre_float[..., hid_units:]
    sigmoid_gate = jax.nn.sigmoid(gate_pre)
    upstream_float = upstream.astype(jnp.float32)
    grad_gate = upstream_float * up_pre * sigmoid_gate * (1.0 + gate_pre * (1.0 - sigmoid_gate))
    grad_up = upstream_float * gate_pre * sigmoid_gate
    return jnp.concatenate([grad_gate, grad_up], axis=-1).astype(jnp.bfloat16)


def make_shards(sections, zs):
    chips = 2 * zs

    def shards(prev_out, fwd_experts, expert_weights, bwd_experts, grad_hidden, saved_pre):
        experts = chips
        capacity = grad_hidden.shape[3]
        hid_units = grad_hidden.shape[4]
        model_width = prev_out.shape[2]
        weights = expert_weights[0, 0]
        core = lax.axis_index("core")
        chip = jnp.arange(chips, dtype=jnp.int32)
        worked = (chip // 2) * 4 + (1 - chip % 2) * 2

        ids = swap_ylo(jnp.concatenate([fwd_experts[0], bwd_experts[0]], axis=1))
        fwd_ids = ids[:, : fwd_experts.shape[2]]
        bwd_ids = ids[:, fwd_experts.shape[2] :]

        rows = lax.ppermute(prev_out[0], RING, ring_route(sections, 1))

        order = jnp.concatenate([worked + core, worked + 1 - core])
        upstream = jnp.take(grad_hidden[0, 0], order, axis=0)
        saved = jnp.take(saved_pre[0, 0], order, axis=0)
        grad_pre = swiglu_backward(upstream, saved).reshape(2, chips, capacity, 2 * hid_units)
        width = model_width // 4
        sums = []
        for cols in [weights[i * width : (i + 1) * width] for i in range(4)]:
            part = jnp.einsum(
                "kech,dh->kecd", grad_pre, cols, preferred_element_type=jnp.float32
            ).astype(jnp.bfloat16)
            other = lax.ppermute(part[1], "core", [(0, 1), (1, 0)])
            sums.append(part[0].astype(jnp.float32) + other.astype(jnp.float32))
        pair_sum = jnp.concatenate(sums, axis=-1).astype(jnp.bfloat16)
        returned = lax.all_to_all(pair_sum, CHIPS, split_axis=0, concat_axis=0, tiled=True)
        rows, returned = lax.optimization_barrier((rows, returned))

        fwd_table = slot_table(fwd_ids, experts, capacity).astype(jnp.bfloat16)
        picked = jnp.einsum(
            "ect,td->ecd", fwd_table, rows, preferred_element_type=jnp.float32
        ).astype(jnp.bfloat16)
        arrived = lax.all_to_all(picked, CHIPS, split_axis=0, concat_axis=0, tiled=True)

        partner = lax.ppermute(arrived, "core", [(0, 1), (1, 0)])
        bwd_table = slot_table(bwd_ids, experts, capacity).astype(jnp.bfloat16)
        grad_in = jnp.einsum(
            "ect,ecd->td", bwd_table, returned, preferred_element_type=jnp.float32
        ).astype(jnp.bfloat16)
        grad_in, partner = lax.optimization_barrier((grad_in, partner))
        grad_rows = lax.ppermute(grad_in, RING, ring_route(sections, -1))

        projected = jnp.einsum(
            "scd,dh->sch",
            jnp.concatenate([arrived, partner]),
            weights,
            preferred_element_type=jnp.float32,
        )
        hidden = (jax.nn.silu(projected[..., :hid_units]) * projected[..., hid_units:]).astype(
            jnp.bfloat16
        )
        blocks = jnp.arange(2 * experts, dtype=jnp.int32)
        chip_of = (blocks // 4) * 2 + (1 - (blocks // 2) % 2)
        hidden = jnp.take(hidden, jnp.where(blocks % 2 == core, chip_of, chips + chip_of), axis=0)
        hidden, grad_rows = lax.optimization_barrier((hidden, grad_rows))
        return (hidden[None, None], grad_rows[None])

    return shards


def solution(mesh):
    sections = mesh.shape["pp"]
    groups = mesh.shape["ep"]
    zs = groups // 4
    devices = np.asarray(mesh.devices).reshape(sections // 2, 2, zs, 2, 2)
    fine = Mesh(devices, PP + EP)
    placed = (
        P(PP, EP, None),
        P(PP, EP, None),
        P(PP, EP, None, None),
        P(PP, EP, None),
        P(PP, EP, None, None, None),
        P(PP, EP, None, None, None),
    )
    return jax.shard_map(
        make_shards(sections, zs),
        mesh=fine,
        in_specs=placed,
        out_specs=(P(PP, EP, None, None, None), P(PP, EP, None)),
        check_vma=False,
    )
```

```python
import numpy as np
import jax
import jax.numpy as jnp
from jax import lax
from jax.sharding import Mesh
from jax.sharding import PartitionSpec as P

PP = ("x", "yhi")
EP = ("z", "ylo", "core")
CHIPS = ("z", "ylo")
RING = ("x", "yhi", "ylo")


def ring_route(sections, distance):
    route = []
    for p in range(sections):
        for lo in range(2):
            route.append((p * 2 + lo, ((p + distance) % sections) * 2 + (1 - lo)))
    return route


def swap_ylo(block):
    return lax.ppermute(block, "ylo", [(0, 1), (1, 0)])


def slot_table(route_ids, expert_count, capacity):
    token_count, choice_count = route_ids.shape
    flattened = route_ids.reshape(token_count * choice_count)
    onehot = (flattened[:, None] == jnp.arange(expert_count, dtype=jnp.int32)[None, :]).astype(
        jnp.int32
    )
    earlier = jnp.cumsum(onehot, axis=0) - onehot
    slot_index = jnp.sum(earlier * onehot, axis=1)
    slot_match = (slot_index[:, None] == jnp.arange(capacity, dtype=jnp.int32)[None, :]).astype(
        jnp.float32
    )
    expert_match = onehot.astype(jnp.float32)
    joined = jnp.einsum("re,rc->rec", expert_match, slot_match).reshape(
        token_count, choice_count, expert_count, capacity
    )
    return jnp.transpose(jnp.sum(joined, axis=1), (1, 2, 0))


def swiglu_backward(upstream, saved):
    hid_units = upstream.shape[-1]
    pre_float = saved.astype(jnp.float32)
    gate_pre = pre_float[..., :hid_units]
    up_pre = pre_float[..., hid_units:]
    sigmoid_gate = jax.nn.sigmoid(gate_pre)
    upstream_float = upstream.astype(jnp.float32)
    grad_gate = upstream_float * up_pre * sigmoid_gate * (1.0 + gate_pre * (1.0 - sigmoid_gate))
    grad_up = upstream_float * gate_pre * sigmoid_gate
    return jnp.concatenate([grad_gate, grad_up], axis=-1).astype(jnp.bfloat16)


def make_shards(sections, zs):
    chips = 2 * zs

    def shards(prev_out, fwd_experts, expert_weights, bwd_experts, grad_hidden, saved_pre):
        experts = chips
        capacity = grad_hidden.shape[3]
        hid_units = grad_hidden.shape[4]
        model_width = prev_out.shape[2]
        weights = expert_weights[0, 0]
        core = lax.axis_index("core")
        chip = jnp.arange(chips, dtype=jnp.int32)
        worked = (chip // 2) * 4 + (1 - chip % 2) * 2

        ids = swap_ylo(jnp.concatenate([fwd_experts[0], bwd_experts[0]], axis=1))
        fwd_ids = ids[:, : fwd_experts.shape[2]]
        bwd_ids = ids[:, fwd_experts.shape[2] :]

        rows = lax.ppermute(prev_out[0], RING, ring_route(sections, 1))

        order = jnp.concatenate([worked + core, worked + 1 - core])
        upstream = jnp.take(grad_hidden[0, 0], order, axis=0)
        saved = jnp.take(saved_pre[0, 0], order, axis=0)
        grad_pre = swiglu_backward(upstream, saved).reshape(2, chips, capacity, 2 * hid_units)
        width = model_width // 2
        sums = []
        for cols in (weights[:width], weights[width:]):
            part = jnp.einsum(
                "kech,dh->kecd", grad_pre, cols, preferred_element_type=jnp.float32
            ).astype(jnp.bfloat16)
            other = lax.ppermute(part[1], "core", [(0, 1), (1, 0)])
            sums.append(part[0].astype(jnp.float32) + other.astype(jnp.float32))
        pair_sum = jnp.concatenate(sums, axis=-1).astype(jnp.bfloat16)
        returned = lax.all_to_all(pair_sum, CHIPS, split_axis=0, concat_axis=0, tiled=True)
        rows, returned = lax.optimization_barrier((rows, returned))

        fwd_table = slot_table(fwd_ids, experts, capacity).astype(jnp.bfloat16)
        picked = jnp.einsum(
            "ect,td->ecd", fwd_table, rows, preferred_element_type=jnp.float32
        ).astype(jnp.bfloat16)
        arrived = lax.all_to_all(picked, CHIPS, split_axis=0, concat_axis=0, tiled=True)

        half = capacity // 2
        partner_a = lax.ppermute(arrived[:, :half], "core", [(0, 1), (1, 0)])
        partner_b = lax.ppermute(arrived[:, half:], "core", [(0, 1), (1, 0)])
        bwd_table = slot_table(bwd_ids, experts, capacity).astype(jnp.bfloat16)
        grad_in = jnp.einsum(
            "ect,ecd->td", bwd_table, returned, preferred_element_type=jnp.float32
        ).astype(jnp.bfloat16)
        grad_in, partner_a = lax.optimization_barrier((grad_in, partner_a))
        grad_rows = lax.ppermute(grad_in, RING, ring_route(sections, -1))

        projected = jnp.concatenate(
            [
                jnp.einsum(
                    "scd,dh->sch",
                    jnp.concatenate([arrived[:, :half], partner_a]),
                    weights,
                    preferred_element_type=jnp.float32,
                ),
                jnp.einsum(
                    "scd,dh->sch",
                    jnp.concatenate([arrived[:, half:], partner_b]),
                    weights,
                    preferred_element_type=jnp.float32,
                ),
            ],
            axis=1,
        )
        hidden = (jax.nn.silu(projected[..., :hid_units]) * projected[..., hid_units:]).astype(
            jnp.bfloat16
        )
        blocks = jnp.arange(2 * experts, dtype=jnp.int32)
        chip_of = (blocks // 4) * 2 + (1 - (blocks // 2) % 2)
        hidden = jnp.take(hidden, jnp.where(blocks % 2 == core, chip_of, chips + chip_of), axis=0)
        hidden, grad_rows = lax.optimization_barrier((hidden, grad_rows))
        return (hidden[None, None], grad_rows[None])

    return shards


def solution(mesh):
    sections = mesh.shape["pp"]
    groups = mesh.shape["ep"]
    zs = groups // 4
    devices = np.asarray(mesh.devices).reshape(sections // 2, 2, zs, 2, 2)
    fine = Mesh(devices, PP + EP)
    placed = (
        P(PP, EP, None),
        P(PP, EP, None),
        P(PP, EP, None, None),
        P(PP, EP, None),
        P(PP, EP, None, None, None),
        P(PP, EP, None, None, None),
    )
    return jax.shard_map(
        make_shards(sections, zs),
        mesh=fine,
        in_specs=placed,
        out_specs=(P(PP, EP, None, None, None), P(PP, EP, None)),
        check_vma=False,
    )
```

```python
import numpy as np
import jax
import jax.numpy as jnp
from jax import lax
from jax.sharding import Mesh
from jax.sharding import PartitionSpec as P

PP = ("x", "yhi")
EP = ("z", "ylo", "core")
CHIPS = ("z", "ylo")
RING = ("x", "yhi", "ylo")


def ring_route(sections, distance):
    route = []
    for p in range(sections):
        for lo in range(2):
            route.append((p * 2 + lo, ((p + distance) % sections) * 2 + (1 - lo)))
    return route


def swap_ylo(block):
    return lax.ppermute(block, "ylo", [(0, 1), (1, 0)])


def slot_table(route_ids, expert_count, capacity):
    token_count, choice_count = route_ids.shape
    flattened = route_ids.reshape(token_count * choice_count)
    onehot = (flattened[:, None] == jnp.arange(expert_count, dtype=jnp.int32)[None, :]).astype(
        jnp.int32
    )
    earlier = jnp.cumsum(onehot, axis=0) - onehot
    slot_index = jnp.sum(earlier * onehot, axis=1)
    slot_match = (slot_index[:, None] == jnp.arange(capacity, dtype=jnp.int32)[None, :]).astype(
        jnp.float32
    )
    expert_match = onehot.astype(jnp.float32)
    joined = jnp.einsum("re,rc->rec", expert_match, slot_match).reshape(
        token_count, choice_count, expert_count, capacity
    )
    return jnp.transpose(jnp.sum(joined, axis=1), (1, 2, 0))


def swiglu_backward(upstream, saved):
    hid_units = upstream.shape[-1]
    pre_float = saved.astype(jnp.float32)
    gate_pre = pre_float[..., :hid_units]
    up_pre = pre_float[..., hid_units:]
    sigmoid_gate = jax.nn.sigmoid(gate_pre)
    upstream_float = upstream.astype(jnp.float32)
    grad_gate = upstream_float * up_pre * sigmoid_gate * (1.0 + gate_pre * (1.0 - sigmoid_gate))
    grad_up = upstream_float * gate_pre * sigmoid_gate
    return jnp.concatenate([grad_gate, grad_up], axis=-1).astype(jnp.bfloat16)


def make_shards(sections, zs):
    chips = 2 * zs

    def shards(prev_out, fwd_experts, expert_weights, bwd_experts, grad_hidden, saved_pre):
        experts = chips
        capacity = grad_hidden.shape[3]
        hid_units = grad_hidden.shape[4]
        model_width = prev_out.shape[2]
        weights = expert_weights[0, 0]
        core = lax.axis_index("core")
        chip = jnp.arange(chips, dtype=jnp.int32)
        worked = (chip // 2) * 4 + (1 - chip % 2) * 2

        ids = swap_ylo(jnp.concatenate([fwd_experts[0], bwd_experts[0]], axis=1))
        fwd_ids = ids[:, : fwd_experts.shape[2]]
        bwd_ids = ids[:, fwd_experts.shape[2] :]

        rows = lax.ppermute(prev_out[0], RING, ring_route(sections, 1))

        order = jnp.concatenate([worked + core, worked + 1 - core])
        upstream = jnp.take(grad_hidden[0, 0], order, axis=0)
        saved = jnp.take(saved_pre[0, 0], order, axis=0)
        grad_pre = swiglu_backward(upstream, saved).reshape(2, chips, capacity, 2 * hid_units)
        width = model_width // 2
        sums = []
        for cols in (weights[:width], weights[width:]):
            part = jnp.einsum(
                "kech,dh->kecd", grad_pre, cols, preferred_element_type=jnp.float32
            ).astype(jnp.bfloat16)
            other = lax.ppermute(part[1], "core", [(0, 1), (1, 0)])
            sums.append(
                (part[0].astype(jnp.float32) + other.astype(jnp.float32)).astype(jnp.bfloat16)
            )
        pair_sum = jnp.concatenate(sums, axis=-1)
        returned = lax.all_to_all(pair_sum, CHIPS, split_axis=0, concat_axis=0, tiled=True)
        rows, returned = lax.optimization_barrier((rows, returned))

        fwd_table = slot_table(fwd_ids, experts, capacity).astype(jnp.bfloat16)
        picked = jnp.einsum(
            "ect,td->ecd", fwd_table, rows, preferred_element_type=jnp.float32
        ).astype(jnp.bfloat16)
        arrived = lax.all_to_all(picked, CHIPS, split_axis=0, concat_axis=0, tiled=True)

        half = capacity // 2
        partner_a = lax.ppermute(arrived[:, :half], "core", [(0, 1), (1, 0)])
        partner_b = lax.ppermute(arrived[:, half:], "core", [(0, 1), (1, 0)])
        bwd_table = slot_table(bwd_ids, experts, capacity).astype(jnp.bfloat16)
        grad_in = jnp.einsum(
            "ect,ecd->td", bwd_table, returned, preferred_element_type=jnp.float32
        ).astype(jnp.bfloat16)
        grad_in, partner_a = lax.optimization_barrier((grad_in, partner_a))
        grad_rows = lax.ppermute(grad_in, RING, ring_route(sections, -1))

        projected = jnp.concatenate(
            [
                jnp.einsum(
                    "scd,dh->sch",
                    jnp.concatenate([arrived[:, :half], partner_a]),
                    weights,
                    preferred_element_type=jnp.float32,
                ),
                jnp.einsum(
                    "scd,dh->sch",
                    jnp.concatenate([arrived[:, half:], partner_b]),
                    weights,
                    preferred_element_type=jnp.float32,
                ),
            ],
            axis=1,
        )
        hidden = (jax.nn.silu(projected[..., :hid_units]) * projected[..., hid_units:]).astype(
            jnp.bfloat16
        )
        blocks = jnp.arange(2 * experts, dtype=jnp.int32)
        chip_of = (blocks // 4) * 2 + (1 - (blocks // 2) % 2)
        hidden = jnp.take(hidden, jnp.where(blocks % 2 == core, chip_of, chips + chip_of), axis=0)
        hidden, grad_rows = lax.optimization_barrier((hidden, grad_rows))
        return (hidden[None, None], grad_rows[None])

    return shards


def solution(mesh):
    sections = mesh.shape["pp"]
    groups = mesh.shape["ep"]
    zs = groups // 4
    devices = np.asarray(mesh.devices).reshape(sections // 2, 2, zs, 2, 2)
    fine = Mesh(devices, PP + EP)
    placed = (
        P(PP, EP, None),
        P(PP, EP, None),
        P(PP, EP, None, None),
        P(PP, EP, None),
        P(PP, EP, None, None, None),
        P(PP, EP, None, None, None),
    )
    return jax.shard_map(
        make_shards(sections, zs),
        mesh=fine,
        in_specs=placed,
        out_specs=(P(PP, EP, None, None, None), P(PP, EP, None)),
        check_vma=False,
    )
```

```python
import numpy as np
import jax
import jax.numpy as jnp
from jax import lax
from jax.sharding import Mesh
from jax.sharding import PartitionSpec as P

PP = ("x", "yhi")
EP = ("z", "ylo", "core")
CHIPS = ("z", "ylo")
RING = ("x", "yhi", "ylo")


def ring_route(sections, distance):
    route = []
    for p in range(sections):
        for lo in range(2):
            route.append((p * 2 + lo, ((p + distance) % sections) * 2 + (1 - lo)))
    return route


def swap_ylo(block):
    return lax.ppermute(block, "ylo", [(0, 1), (1, 0)])


def slot_table(route_ids, expert_count, capacity):
    token_count, choice_count = route_ids.shape
    flattened = route_ids.reshape(token_count * choice_count)
    onehot = (flattened[:, None] == jnp.arange(expert_count, dtype=jnp.int32)[None, :]).astype(
        jnp.int32
    )
    earlier = jnp.cumsum(onehot, axis=0) - onehot
    slot_index = jnp.sum(earlier * onehot, axis=1)
    slot_match = (slot_index[:, None] == jnp.arange(capacity, dtype=jnp.int32)[None, :]).astype(
        jnp.float32
    )
    expert_match = onehot.astype(jnp.float32)
    joined = jnp.einsum("re,rc->rec", expert_match, slot_match).reshape(
        token_count, choice_count, expert_count, capacity
    )
    return jnp.transpose(jnp.sum(joined, axis=1), (1, 2, 0))


def swiglu_backward(upstream, saved):
    hid_units = upstream.shape[-1]
    pre_float = saved.astype(jnp.float32)
    gate_pre = pre_float[..., :hid_units]
    up_pre = pre_float[..., hid_units:]
    sigmoid_gate = jax.nn.sigmoid(gate_pre)
    upstream_float = upstream.astype(jnp.float32)
    grad_gate = upstream_float * up_pre * sigmoid_gate * (1.0 + gate_pre * (1.0 - sigmoid_gate))
    grad_up = upstream_float * gate_pre * sigmoid_gate
    return jnp.concatenate([grad_gate, grad_up], axis=-1).astype(jnp.bfloat16)


def make_shards(sections, zs):
    chips = 2 * zs

    def shards(prev_out, fwd_experts, expert_weights, bwd_experts, grad_hidden, saved_pre):
        experts = chips
        capacity = grad_hidden.shape[3]
        hid_units = grad_hidden.shape[4]
        model_width = prev_out.shape[2]
        weights = expert_weights[0, 0]
        core = lax.axis_index("core")
        chip = jnp.arange(chips, dtype=jnp.int32)
        worked = (chip // 2) * 4 + (1 - chip % 2) * 2

        ids = swap_ylo(jnp.concatenate([fwd_experts[0], bwd_experts[0]], axis=1))
        fwd_ids = ids[:, : fwd_experts.shape[2]]
        bwd_ids = ids[:, fwd_experts.shape[2] :]

        rows = lax.ppermute(prev_out[0], RING, ring_route(sections, 1))

        order = jnp.concatenate([worked + core, worked + 1 - core])
        upstream = jnp.take(grad_hidden[0, 0], order, axis=0)
        saved = jnp.take(saved_pre[0, 0], order, axis=0)
        grad_pre = swiglu_backward(upstream, saved).reshape(2, chips, capacity, 2 * hid_units)
        width = model_width // 2
        sums = []
        for cols in (weights[:width], weights[width:]):
            part = jnp.einsum(
                "kech,dh->kecd", grad_pre, cols, preferred_element_type=jnp.float32
            ).astype(jnp.bfloat16)
            other = lax.ppermute(part[1], "core", [(0, 1), (1, 0)])
            sums.append(part[0].astype(jnp.float32) + other.astype(jnp.float32))
        pair_sum = jnp.concatenate(sums, axis=-1).astype(jnp.bfloat16)
        returned = lax.all_to_all(pair_sum, CHIPS, split_axis=0, concat_axis=0, tiled=True)
        rows, returned = lax.optimization_barrier((rows, returned))

        fwd_table = slot_table(fwd_ids, experts, capacity).astype(jnp.bfloat16)
        half = capacity // 2
        arrived_ab = [
            lax.all_to_all(
                jnp.einsum(
                    "ect,td->ecd", table_half, rows, preferred_element_type=jnp.float32
                ).astype(jnp.bfloat16),
                CHIPS,
                split_axis=0,
                concat_axis=0,
                tiled=True,
            )
            for table_half in (fwd_table[:, :half], fwd_table[:, half:])
        ]
        partner_a = lax.ppermute(arrived_ab[0], "core", [(0, 1), (1, 0)])
        partner_b = lax.ppermute(arrived_ab[1], "core", [(0, 1), (1, 0)])
        bwd_table = slot_table(bwd_ids, experts, capacity).astype(jnp.bfloat16)
        grad_in = jnp.einsum(
            "ect,ecd->td", bwd_table, returned, preferred_element_type=jnp.float32
        ).astype(jnp.bfloat16)
        grad_in, partner_a = lax.optimization_barrier((grad_in, partner_a))
        grad_rows = lax.ppermute(grad_in, RING, ring_route(sections, -1))

        projected = jnp.concatenate(
            [
                jnp.einsum(
                    "scd,dh->sch",
                    jnp.concatenate([arrived_ab[0], partner_a]),
                    weights,
                    preferred_element_type=jnp.float32,
                ),
                jnp.einsum(
                    "scd,dh->sch",
                    jnp.concatenate([arrived_ab[1], partner_b]),
                    weights,
                    preferred_element_type=jnp.float32,
                ),
            ],
            axis=1,
        )
        hidden = (jax.nn.silu(projected[..., :hid_units]) * projected[..., hid_units:]).astype(
            jnp.bfloat16
        )
        blocks = jnp.arange(2 * experts, dtype=jnp.int32)
        chip_of = (blocks // 4) * 2 + (1 - (blocks // 2) % 2)
        hidden = jnp.take(hidden, jnp.where(blocks % 2 == core, chip_of, chips + chip_of), axis=0)
        hidden, grad_rows = lax.optimization_barrier((hidden, grad_rows))
        return (hidden[None, None], grad_rows[None])

    return shards


def solution(mesh):
    sections = mesh.shape["pp"]
    groups = mesh.shape["ep"]
    zs = groups // 4
    devices = np.asarray(mesh.devices).reshape(sections // 2, 2, zs, 2, 2)
    fine = Mesh(devices, PP + EP)
    placed = (
        P(PP, EP, None),
        P(PP, EP, None),
        P(PP, EP, None, None),
        P(PP, EP, None),
        P(PP, EP, None, None, None),
        P(PP, EP, None, None, None),
    )
    return jax.shard_map(
        make_shards(sections, zs),
        mesh=fine,
        in_specs=placed,
        out_specs=(P(PP, EP, None, None, None), P(PP, EP, None)),
        check_vma=False,
    )
```

```python
import numpy as np
import jax
import jax.numpy as jnp
from jax import lax
from jax.sharding import Mesh
from jax.sharding import PartitionSpec as P

PP = ("x", "yhi")
EP = ("z", "ylo", "core")
CHIPS = ("z", "ylo")
RING = ("x", "yhi", "ylo")


def ring_route(sections, distance):
    route = []
    for p in range(sections):
        for lo in range(2):
            route.append((p * 2 + lo, ((p + distance) % sections) * 2 + (1 - lo)))
    return route


def swap_ylo(block):
    return lax.ppermute(block, "ylo", [(0, 1), (1, 0)])


def slot_table(route_ids, expert_count, capacity):
    token_count, choice_count = route_ids.shape
    flattened = route_ids.reshape(token_count * choice_count)
    onehot = (flattened[:, None] == jnp.arange(expert_count, dtype=jnp.int32)[None, :]).astype(
        jnp.int32
    )
    earlier = jnp.cumsum(onehot, axis=0) - onehot
    slot_index = jnp.sum(earlier * onehot, axis=1)
    slot_match = (slot_index[:, None] == jnp.arange(capacity, dtype=jnp.int32)[None, :]).astype(
        jnp.float32
    )
    expert_match = onehot.astype(jnp.float32)
    joined = jnp.einsum("re,rc->rec", expert_match, slot_match).reshape(
        token_count, choice_count, expert_count, capacity
    )
    return jnp.transpose(jnp.sum(joined, axis=1), (1, 2, 0))


def swiglu_backward(upstream, saved):
    hid_units = upstream.shape[-1]
    pre_float = saved.astype(jnp.float32)
    gate_pre = pre_float[..., :hid_units]
    up_pre = pre_float[..., hid_units:]
    sigmoid_gate = jax.nn.sigmoid(gate_pre)
    upstream_float = upstream.astype(jnp.float32)
    grad_gate = upstream_float * up_pre * sigmoid_gate * (1.0 + gate_pre * (1.0 - sigmoid_gate))
    grad_up = upstream_float * gate_pre * sigmoid_gate
    return jnp.concatenate([grad_gate, grad_up], axis=-1).astype(jnp.bfloat16)


def make_shards(sections, zs):
    chips = 2 * zs

    def shards(prev_out, fwd_experts, expert_weights, bwd_experts, grad_hidden, saved_pre):
        experts = chips
        capacity = grad_hidden.shape[3]
        hid_units = grad_hidden.shape[4]
        model_width = prev_out.shape[2]
        weights = expert_weights[0, 0]
        core = lax.axis_index("core")
        chip = jnp.arange(chips, dtype=jnp.int32)
        worked = (chip // 2) * 4 + (1 - chip % 2) * 2

        ids = swap_ylo(jnp.concatenate([fwd_experts[0], bwd_experts[0]], axis=1))
        fwd_ids = ids[:, : fwd_experts.shape[2]]
        bwd_ids = ids[:, fwd_experts.shape[2] :]

        rows = lax.ppermute(prev_out[0], RING, ring_route(sections, 1))

        order = jnp.concatenate([worked + core, worked + 1 - core])
        upstream = jnp.take(grad_hidden[0, 0], order, axis=0)
        saved = jnp.take(saved_pre[0, 0], order, axis=0)
        grad_pre = swiglu_backward(upstream, saved).reshape(2, chips, capacity, 2 * hid_units)
        width = model_width // 2
        sums = []
        for cols in (weights[:width], weights[width:]):
            part = jnp.einsum(
                "kech,dh->kecd", grad_pre, cols, preferred_element_type=jnp.float32
            ).astype(jnp.bfloat16)
            other = lax.ppermute(part[1], "core", [(0, 1), (1, 0)])
            sums.append(part[0].astype(jnp.float32) + other.astype(jnp.float32))
        pair_sum = jnp.concatenate(sums, axis=-1).astype(jnp.bfloat16)
        returned = lax.all_to_all(pair_sum, CHIPS, split_axis=0, concat_axis=0, tiled=True)
        rows, returned = lax.optimization_barrier((rows, returned))

        fwd_table = slot_table(fwd_ids, experts, capacity).astype(jnp.bfloat16)
        picked = jnp.einsum(
            "ect,td->ecd", fwd_table, rows, preferred_element_type=jnp.float32
        ).astype(jnp.bfloat16)
        arrived = lax.all_to_all(picked, CHIPS, split_axis=0, concat_axis=0, tiled=True)

        half = chips // 2
        partner_a = lax.ppermute(arrived[:half], "core", [(0, 1), (1, 0)])
        partner_b = lax.ppermute(arrived[half:], "core", [(0, 1), (1, 0)])
        bwd_table = slot_table(bwd_ids, experts, capacity).astype(jnp.bfloat16)
        grad_in = jnp.einsum(
            "ect,ecd->td", bwd_table, returned, preferred_element_type=jnp.float32
        ).astype(jnp.bfloat16)
        grad_in, partner_a = lax.optimization_barrier((grad_in, partner_a))
        grad_rows = lax.ppermute(grad_in, RING, ring_route(sections, -1))

        projected = jnp.concatenate(
            [
                jnp.einsum(
                    "scd,dh->sch",
                    jnp.concatenate([arrived[:half], partner_a]),
                    weights,
                    preferred_element_type=jnp.float32,
                ),
                jnp.einsum(
                    "scd,dh->sch",
                    jnp.concatenate([arrived[half:], partner_b]),
                    weights,
                    preferred_element_type=jnp.float32,
                ),
            ],
            axis=0,
        )
        hidden = (jax.nn.silu(projected[..., :hid_units]) * projected[..., hid_units:]).astype(
            jnp.bfloat16
        )
        blocks = jnp.arange(2 * experts, dtype=jnp.int32)
        chip_of = (blocks // 4) * 2 + (1 - (blocks // 2) % 2)
        place = (chip_of // half) * chips + jnp.where(blocks % 2 == core, 0, half) + chip_of % half
        hidden = jnp.take(hidden, place, axis=0)
        hidden, grad_rows = lax.optimization_barrier((hidden, grad_rows))
        return (hidden[None, None], grad_rows[None])

    return shards


def solution(mesh):
    sections = mesh.shape["pp"]
    groups = mesh.shape["ep"]
    zs = groups // 4
    devices = np.asarray(mesh.devices).reshape(sections // 2, 2, zs, 2, 2)
    fine = Mesh(devices, PP + EP)
    placed = (
        P(PP, EP, None),
        P(PP, EP, None),
        P(PP, EP, None, None),
        P(PP, EP, None),
        P(PP, EP, None, None, None),
        P(PP, EP, None, None, None),
    )
    return jax.shard_map(
        make_shards(sections, zs),
        mesh=fine,
        in_specs=placed,
        out_specs=(P(PP, EP, None, None, None), P(PP, EP, None)),
        check_vma=False,
    )
```

```python
import numpy as np
import jax
import jax.numpy as jnp
from jax import lax
from jax.sharding import Mesh
from jax.sharding import PartitionSpec as P

PP = ("x", "yhi")
EP = ("z", "ylo", "core")
CHIPS = ("z", "ylo")
RING = ("x", "yhi", "ylo")


def ring_route(sections, distance):
    route = []
    for p in range(sections):
        for lo in range(2):
            route.append((p * 2 + lo, ((p + distance) % sections) * 2 + (1 - lo)))
    return route


def swap_ylo(block):
    return lax.ppermute(block, "ylo", [(0, 1), (1, 0)])


def slot_table(route_ids, expert_count, capacity):
    token_count, choice_count = route_ids.shape
    flattened = route_ids.reshape(token_count * choice_count)
    onehot = (flattened[:, None] == jnp.arange(expert_count, dtype=jnp.int32)[None, :]).astype(
        jnp.int32
    )
    earlier = jnp.cumsum(onehot, axis=0) - onehot
    slot_index = jnp.sum(earlier * onehot, axis=1)
    slot_match = (slot_index[:, None] == jnp.arange(capacity, dtype=jnp.int32)[None, :]).astype(
        jnp.float32
    )
    expert_match = onehot.astype(jnp.float32)
    joined = jnp.einsum("re,rc->rec", expert_match, slot_match).reshape(
        token_count, choice_count, expert_count, capacity
    )
    return jnp.transpose(jnp.sum(joined, axis=1), (1, 2, 0))


def swiglu_backward(upstream, saved):
    hid_units = upstream.shape[-1]
    pre_float = saved.astype(jnp.float32)
    gate_pre = pre_float[..., :hid_units]
    up_pre = pre_float[..., hid_units:]
    sigmoid_gate = jax.nn.sigmoid(gate_pre)
    upstream_float = upstream.astype(jnp.float32)
    grad_gate = upstream_float * up_pre * sigmoid_gate * (1.0 + gate_pre * (1.0 - sigmoid_gate))
    grad_up = upstream_float * gate_pre * sigmoid_gate
    return jnp.concatenate([grad_gate, grad_up], axis=-1).astype(jnp.bfloat16)


def make_shards(sections, zs):
    chips = 2 * zs

    def shards(prev_out, fwd_experts, expert_weights, bwd_experts, grad_hidden, saved_pre):
        experts = chips
        capacity = grad_hidden.shape[3]
        hid_units = grad_hidden.shape[4]
        model_width = prev_out.shape[2]
        weights = expert_weights[0, 0]
        core = lax.axis_index("core")
        chip = jnp.arange(chips, dtype=jnp.int32)
        worked = (chip // 2) * 4 + (1 - chip % 2) * 2

        ids = swap_ylo(jnp.concatenate([fwd_experts[0], bwd_experts[0]], axis=1))
        fwd_ids = ids[:, : fwd_experts.shape[2]]
        bwd_ids = ids[:, fwd_experts.shape[2] :]

        rows = lax.ppermute(prev_out[0], RING, ring_route(sections, 1))

        order = jnp.concatenate([worked + core, worked + 1 - core])
        upstream = jnp.take(grad_hidden[0, 0], order, axis=0)
        saved = jnp.take(saved_pre[0, 0], order, axis=0)
        grad_pre = swiglu_backward(upstream, saved).reshape(2, chips, capacity, 2 * hid_units)
        width = model_width // 2
        sums = []
        for cols in (weights[:width], weights[width:]):
            part = jnp.einsum(
                "kech,dh->kecd", grad_pre, cols, preferred_element_type=jnp.float32
            ).astype(jnp.bfloat16)
            other = lax.ppermute(part[1], "core", [(0, 1), (1, 0)])
            sums.append(part[0].astype(jnp.float32) + other.astype(jnp.float32))
        pair_sum = jnp.concatenate(sums, axis=-1).astype(jnp.bfloat16)
        returned = lax.all_to_all(pair_sum, CHIPS, split_axis=0, concat_axis=0, tiled=True)
        rows, returned = lax.optimization_barrier((rows, returned))

        fwd_table = slot_table(fwd_ids, experts, capacity).astype(jnp.bfloat16)
        picked = jnp.einsum(
            "ect,td->ecd", fwd_table, rows, preferred_element_type=jnp.float32
        ).astype(jnp.bfloat16)
        arrived = lax.all_to_all(picked, CHIPS, split_axis=0, concat_axis=0, tiled=True)

        half = chips // 2
        partner_a = lax.ppermute(arrived[:half], "core", [(0, 1), (1, 0)])
        partner_b = lax.ppermute(arrived[half:], "core", [(0, 1), (1, 0)])
        bwd_table = slot_table(bwd_ids, experts, capacity).astype(jnp.bfloat16)
        grad_in = [
            jnp.einsum(
                "ect,ecd->td", bwd_table, returned[..., start : start + width],
                preferred_element_type=jnp.float32,
            ).astype(jnp.bfloat16)
            for start in (0, width)
        ]
        first, partner_a = lax.optimization_barrier((grad_in[0], partner_a))
        grad_rows = jnp.concatenate(
            [
                lax.ppermute(first, RING, ring_route(sections, -1)),
                lax.ppermute(grad_in[1], RING, ring_route(sections, -1)),
            ],
            axis=-1,
        )

        projected = jnp.concatenate(
            [
                jnp.einsum(
                    "scd,dh->sch",
                    jnp.concatenate([arrived[:half], partner_a]),
                    weights,
                    preferred_element_type=jnp.float32,
                ),
                jnp.einsum(
                    "scd,dh->sch",
                    jnp.concatenate([arrived[half:], partner_b]),
                    weights,
                    preferred_element_type=jnp.float32,
                ),
            ],
            axis=0,
        )
        hidden = (jax.nn.silu(projected[..., :hid_units]) * projected[..., hid_units:]).astype(
            jnp.bfloat16
        )
        blocks = jnp.arange(2 * experts, dtype=jnp.int32)
        chip_of = (blocks // 4) * 2 + (1 - (blocks // 2) % 2)
        place = (chip_of // half) * chips + jnp.where(blocks % 2 == core, 0, half) + chip_of % half
        hidden = jnp.take(hidden, place, axis=0)
        hidden, grad_rows = lax.optimization_barrier((hidden, grad_rows))
        return (hidden[None, None], grad_rows[None])

    return shards


def solution(mesh):
    sections = mesh.shape["pp"]
    groups = mesh.shape["ep"]
    zs = groups // 4
    devices = np.asarray(mesh.devices).reshape(sections // 2, 2, zs, 2, 2)
    fine = Mesh(devices, PP + EP)
    placed = (
        P(PP, EP, None),
        P(PP, EP, None),
        P(PP, EP, None, None),
        P(PP, EP, None),
        P(PP, EP, None, None, None),
        P(PP, EP, None, None, None),
    )
    return jax.shard_map(
        make_shards(sections, zs),
        mesh=fine,
        in_specs=placed,
        out_specs=(P(PP, EP, None, None, None), P(PP, EP, None)),
        check_vma=False,
    )
```

```python
import numpy as np
import jax
import jax.numpy as jnp
from jax import lax
from jax.sharding import Mesh
from jax.sharding import PartitionSpec as P

PP = ("x", "yhi")
EP = ("z", "ylo", "core")
CHIPS = ("z", "ylo")
RING = ("x", "yhi", "ylo")


def ring_route(sections, distance):
    route = []
    for p in range(sections):
        for lo in range(2):
            route.append((p * 2 + lo, ((p + distance) % sections) * 2 + (1 - lo)))
    return route


def swap_ylo(block):
    return lax.ppermute(block, "ylo", [(0, 1), (1, 0)])


def slot_table(route_ids, expert_count, capacity):
    token_count, choice_count = route_ids.shape
    flattened = route_ids.reshape(token_count * choice_count)
    onehot = (flattened[:, None] == jnp.arange(expert_count, dtype=jnp.int32)[None, :]).astype(
        jnp.int32
    )
    earlier = jnp.cumsum(onehot, axis=0) - onehot
    slot_index = jnp.sum(earlier * onehot, axis=1)
    slot_match = (slot_index[:, None] == jnp.arange(capacity, dtype=jnp.int32)[None, :]).astype(
        jnp.float32
    )
    expert_match = onehot.astype(jnp.float32)
    joined = jnp.einsum("re,rc->rec", expert_match, slot_match).reshape(
        token_count, choice_count, expert_count, capacity
    )
    return jnp.transpose(jnp.sum(joined, axis=1), (1, 2, 0))


def swiglu_backward(upstream, saved):
    hid_units = upstream.shape[-1]
    pre_float = saved.astype(jnp.float32)
    gate_pre = pre_float[..., :hid_units]
    up_pre = pre_float[..., hid_units:]
    sigmoid_gate = jax.nn.sigmoid(gate_pre)
    upstream_float = upstream.astype(jnp.float32)
    grad_gate = upstream_float * up_pre * sigmoid_gate * (1.0 + gate_pre * (1.0 - sigmoid_gate))
    grad_up = upstream_float * gate_pre * sigmoid_gate
    return jnp.concatenate([grad_gate, grad_up], axis=-1).astype(jnp.bfloat16)


def make_shards(sections, zs):
    chips = 2 * zs

    def shards(prev_out, fwd_experts, expert_weights, bwd_experts, grad_hidden, saved_pre):
        experts = chips
        capacity = grad_hidden.shape[3]
        hid_units = grad_hidden.shape[4]
        model_width = prev_out.shape[2]
        weights = expert_weights[0, 0]
        core = lax.axis_index("core")
        chip = jnp.arange(chips, dtype=jnp.int32)
        worked = (chip // 2) * 4 + (1 - chip % 2) * 2

        ids = swap_ylo(jnp.concatenate([fwd_experts[0], bwd_experts[0]], axis=1))
        fwd_ids = ids[:, : fwd_experts.shape[2]]
        bwd_ids = ids[:, fwd_experts.shape[2] :]

        rows = lax.ppermute(prev_out[0], RING, ring_route(sections, 1))

        order = jnp.concatenate([worked + core, worked + 1 - core])
        upstream = jnp.take(grad_hidden[0, 0], order, axis=0)
        saved = jnp.take(saved_pre[0, 0], order, axis=0)
        grad_pre = swiglu_backward(upstream, saved).reshape(2, chips, capacity, 2 * hid_units)
        width = model_width // 2
        sums = []
        for cols in (weights[:width], weights[width:]):
            part = jnp.einsum(
                "kech,dh->kecd", grad_pre, cols, preferred_element_type=jnp.float32
            ).astype(jnp.bfloat16)
            other = lax.ppermute(part[1], "core", [(0, 1), (1, 0)])
            sums.append(part[0].astype(jnp.float32) + other.astype(jnp.float32))
        pair_sum = jnp.concatenate(sums, axis=-1).astype(jnp.bfloat16)
        returned = lax.all_to_all(pair_sum, CHIPS, split_axis=0, concat_axis=0, tiled=True)
        rows, returned = lax.optimization_barrier((rows, returned))

        fwd_table = slot_table(fwd_ids, experts, capacity).astype(jnp.bfloat16)
        picked = jnp.einsum(
            "ect,td->ecd", fwd_table, rows, preferred_element_type=jnp.float32
        ).astype(jnp.bfloat16)
        arrived = lax.all_to_all(picked, CHIPS, split_axis=0, concat_axis=0, tiled=True)

        half = chips // 2
        partner_a = lax.ppermute(arrived[:half], "core", [(0, 1), (1, 0)])
        partner_b = lax.ppermute(arrived[half:], "core", [(0, 1), (1, 0)])
        bwd_table = slot_table(bwd_ids, experts, capacity).astype(jnp.bfloat16)
        piece = model_width // 4
        grad_in = [
            jnp.einsum(
                "ect,ecd->td", bwd_table, returned[..., start : start + piece],
                preferred_element_type=jnp.float32,
            ).astype(jnp.bfloat16)
            for start in range(0, model_width, piece)
        ]
        grad_in[0], partner_a = lax.optimization_barrier((grad_in[0], partner_a))
        grad_rows = jnp.concatenate(
            [lax.ppermute(g, RING, ring_route(sections, -1)) for g in grad_in], axis=-1
        )

        projected = jnp.concatenate(
            [
                jnp.einsum(
                    "scd,dh->sch",
                    jnp.concatenate([arrived[:half], partner_a]),
                    weights,
                    preferred_element_type=jnp.float32,
                ),
                jnp.einsum(
                    "scd,dh->sch",
                    jnp.concatenate([arrived[half:], partner_b]),
                    weights,
                    preferred_element_type=jnp.float32,
                ),
            ],
            axis=0,
        )
        hidden = (jax.nn.silu(projected[..., :hid_units]) * projected[..., hid_units:]).astype(
            jnp.bfloat16
        )
        blocks = jnp.arange(2 * experts, dtype=jnp.int32)
        chip_of = (blocks // 4) * 2 + (1 - (blocks // 2) % 2)
        place = (chip_of // half) * chips + jnp.where(blocks % 2 == core, 0, half) + chip_of % half
        hidden = jnp.take(hidden, place, axis=0)
        hidden, grad_rows = lax.optimization_barrier((hidden, grad_rows))
        return (hidden[None, None], grad_rows[None])

    return shards


def solution(mesh):
    sections = mesh.shape["pp"]
    groups = mesh.shape["ep"]
    zs = groups // 4
    devices = np.asarray(mesh.devices).reshape(sections // 2, 2, zs, 2, 2)
    fine = Mesh(devices, PP + EP)
    placed = (
        P(PP, EP, None),
        P(PP, EP, None),
        P(PP, EP, None, None),
        P(PP, EP, None),
        P(PP, EP, None, None, None),
        P(PP, EP, None, None, None),
    )
    return jax.shard_map(
        make_shards(sections, zs),
        mesh=fine,
        in_specs=placed,
        out_specs=(P(PP, EP, None, None, None), P(PP, EP, None)),
        check_vma=False,
    )
```

```python
import numpy as np
import jax
import jax.numpy as jnp
from jax import lax
from jax.sharding import Mesh
from jax.sharding import PartitionSpec as P

PP = ("x", "yhi")
EP = ("z", "ylo", "core")
CHIPS = ("z", "ylo")
RING = ("x", "yhi", "ylo")


def ring_route(sections, distance):
    route = []
    for p in range(sections):
        for lo in range(2):
            route.append((p * 2 + lo, ((p + distance) % sections) * 2 + (1 - lo)))
    return route


def swap_ylo(block):
    return lax.ppermute(block, "ylo", [(0, 1), (1, 0)])


def slot_table(route_ids, expert_count, capacity):
    token_count, choice_count = route_ids.shape
    flattened = route_ids.reshape(token_count * choice_count)
    onehot = (flattened[:, None] == jnp.arange(expert_count, dtype=jnp.int32)[None, :]).astype(
        jnp.int32
    )
    earlier = jnp.cumsum(onehot, axis=0) - onehot
    slot_index = jnp.sum(earlier * onehot, axis=1)
    slot_match = (slot_index[:, None] == jnp.arange(capacity, dtype=jnp.int32)[None, :]).astype(
        jnp.float32
    )
    expert_match = onehot.astype(jnp.float32)
    joined = jnp.einsum("re,rc->rec", expert_match, slot_match).reshape(
        token_count, choice_count, expert_count, capacity
    )
    return jnp.transpose(jnp.sum(joined, axis=1), (1, 2, 0))


def swiglu_backward(upstream, saved):
    hid_units = upstream.shape[-1]
    pre_float = saved.astype(jnp.float32)
    gate_pre = pre_float[..., :hid_units]
    up_pre = pre_float[..., hid_units:]
    sigmoid_gate = jax.nn.sigmoid(gate_pre)
    upstream_float = upstream.astype(jnp.float32)
    grad_gate = upstream_float * up_pre * sigmoid_gate * (1.0 + gate_pre * (1.0 - sigmoid_gate))
    grad_up = upstream_float * gate_pre * sigmoid_gate
    return jnp.concatenate([grad_gate, grad_up], axis=-1).astype(jnp.bfloat16)


def make_shards(sections, zs):
    chips = 2 * zs

    def shards(prev_out, fwd_experts, expert_weights, bwd_experts, grad_hidden, saved_pre):
        experts = chips
        capacity = grad_hidden.shape[3]
        hid_units = grad_hidden.shape[4]
        model_width = prev_out.shape[2]
        weights = expert_weights[0, 0]
        core = lax.axis_index("core")
        chip = jnp.arange(chips, dtype=jnp.int32)
        worked = (chip // 2) * 4 + (1 - chip % 2) * 2

        ids = swap_ylo(jnp.concatenate([fwd_experts[0], bwd_experts[0]], axis=1))
        fwd_ids = ids[:, : fwd_experts.shape[2]]
        bwd_ids = ids[:, fwd_experts.shape[2] :]

        rows = lax.ppermute(prev_out[0], RING, ring_route(sections, 1))

        order = jnp.concatenate([worked + core, worked + 1 - core])
        upstream = jnp.take(grad_hidden[0, 0], order, axis=0)
        saved = jnp.take(saved_pre[0, 0], order, axis=0)
        grad_pre = swiglu_backward(upstream, saved).reshape(2, chips, capacity, 2 * hid_units)
        width = model_width // 2
        sums = []
        for cols in (weights[:width], weights[width:]):
            part = jnp.einsum(
                "kech,dh->kecd", grad_pre, cols, preferred_element_type=jnp.float32
            ).astype(jnp.bfloat16)
            other = lax.ppermute(part[1], "core", [(0, 1), (1, 0)])
            sums.append(part[0].astype(jnp.float32) + other.astype(jnp.float32))
        pair_sum = jnp.concatenate(sums, axis=-1).astype(jnp.bfloat16)
        returned = lax.all_to_all(pair_sum, CHIPS, split_axis=0, concat_axis=0, tiled=True)
        rows, returned = lax.optimization_barrier((rows, returned))

        fwd_table = slot_table(fwd_ids, experts, capacity).astype(jnp.bfloat16)
        picked = jnp.einsum(
            "ect,td->ecd", fwd_table, rows, preferred_element_type=jnp.float32
        ).astype(jnp.bfloat16)
        arrived = lax.all_to_all(picked, CHIPS, split_axis=0, concat_axis=0, tiled=True)

        half = chips // 2
        partner_a = lax.ppermute(arrived[:half], "core", [(0, 1), (1, 0)])
        partner_b = lax.ppermute(arrived[half:], "core", [(0, 1), (1, 0)])
        bwd_table = slot_table(bwd_ids, experts, capacity).astype(jnp.bfloat16)
        grad_in = [
            jnp.einsum(
                "ect,ecd->td", bwd_table, returned[..., start : start + width],
                preferred_element_type=jnp.float32,
            ).astype(jnp.bfloat16)
            for start in (0, width)
        ]
        second, partner_a = lax.optimization_barrier((grad_in[1], partner_a))
        grad_rows = jnp.concatenate(
            [
                lax.ppermute(grad_in[0], RING, ring_route(sections, -1)),
                lax.ppermute(second, RING, ring_route(sections, -1)),
            ],
            axis=-1,
        )

        projected = jnp.concatenate(
            [
                jnp.einsum(
                    "scd,dh->sch",
                    jnp.concatenate([arrived[:half], partner_a]),
                    weights,
                    preferred_element_type=jnp.float32,
                ),
                jnp.einsum(
                    "scd,dh->sch",
                    jnp.concatenate([arrived[half:], partner_b]),
                    weights,
                    preferred_element_type=jnp.float32,
                ),
            ],
            axis=0,
        )
        hidden = (jax.nn.silu(projected[..., :hid_units]) * projected[..., hid_units:]).astype(
            jnp.bfloat16
        )
        blocks = jnp.arange(2 * experts, dtype=jnp.int32)
        chip_of = (blocks // 4) * 2 + (1 - (blocks // 2) % 2)
        place = (chip_of // half) * chips + jnp.where(blocks % 2 == core, 0, half) + chip_of % half
        hidden = jnp.take(hidden, place, axis=0)
        hidden, grad_rows = lax.optimization_barrier((hidden, grad_rows))
        return (hidden[None, None], grad_rows[None])

    return shards


def solution(mesh):
    sections = mesh.shape["pp"]
    groups = mesh.shape["ep"]
    zs = groups // 4
    devices = np.asarray(mesh.devices).reshape(sections // 2, 2, zs, 2, 2)
    fine = Mesh(devices, PP + EP)
    placed = (
        P(PP, EP, None),
        P(PP, EP, None),
        P(PP, EP, None, None),
        P(PP, EP, None),
        P(PP, EP, None, None, None),
        P(PP, EP, None, None, None),
    )
    return jax.shard_map(
        make_shards(sections, zs),
        mesh=fine,
        in_specs=placed,
        out_specs=(P(PP, EP, None, None, None), P(PP, EP, None)),
        check_vma=False,
    )
```
